128 devices in a mesh: row: 8 (over z, core), col: 16 (over y, x).
Axes of the slice: x: 4, y: 4, z: 4, core: 2. Of those that a mesh axis runs over, the one named last changes fastest.
Arguments:
- u_factors: bfloat16 [16, 16, 192, 1024], P('row', 'col'), may hold values from -4 to 4
- v_factors: bfloat16 [16, 16, 192, 1024], P('row', 'col'), may hold values from -4 to 4
- diag_tiles: float32 [16, 1024, 1024], P('row', 'col'), as said below
- sketch: bfloat16 [192, 1024], replicated, may hold values from -1 to 1
- rank_levels: int32 [3, 16, 16], P(None, 'row', 'col'), may hold values from 64 to 192, as said below
Outputs:
- u_out: bfloat16 [16, 16, 192, 1024], P('row', 'col')
- v_out: bfloat16 [16, 16, 192, 1024], P('row', 'col')
- diag_out: float32 [16, 1024, 1024], P('row', 'col')
The draws below stay inside these ranges and needn't reach their ends.
Inputs may be any that keep to these rules, and one draw needn't show every extreme that they name: Every entry is a multiple of 64; rank_levels[l + 1] <= rank_levels[l] entrywise; some tile (i, j) with i > j >= 2 has 192 at every level. `diag_tiles`: each tile is symmetric with eigenvalues between 2 and 20.
All inputs are finite; a program needn't handle non-finite values.
Results may differ from the reference program's by a relative error of at most 0.035.
Values may be sent and summed in bfloat16 or wider, within the bound.
No kernel may reach another device: no remote copies, remote signals or barrier semaphores. Data moves between devices by JAX's collectives and lax.ppermute only.
A program may use at most 128 MiB of HBM per device.

```python
import math
import jax
import jax.numpy as jnp
from jax import lax

B = 1024
BUCKET = 64
PANELS = 2
TR = 2
RMAX = 192
NT = 16
TC = 1
N_ROW = 8
N_COL = 16


def walsh_sign(left_index, right_index):
    common_bits = jnp.bitwise_and(left_index, right_index)
    parity = jnp.zeros_like(common_bits)
    for bit_place in range(B.bit_length()):
        parity = parity + jnp.bitwise_and(jnp.right_shift(common_bits, bit_place), 1)
    return 1.0 - 2.0 * (parity % 2).astype(jnp.float32)


def support_order(key):
    return jax.random.permutation(jax.random.fold_in(key, 101), B).astype(jnp.int32)


def mixing_table(key):
    sign_key, turn_key, order_key = jax.random.split(jax.random.fold_in(key, 57), 3)
    slots = jnp.arange(RMAX, dtype=jnp.int32)
    source_rows = jax.random.permutation(order_key, RMAX).astype(jnp.int32)[:, None]
    target_cols = slots[None, :]
    hadamard_part = walsh_sign(source_rows // 3, target_cols // 3) / math.sqrt(BUCKET)
    small_part = jnp.where(source_rows % 3 == target_cols % 3, -1.0, 2.0) / 3.0
    row_signs = 1.0 - 2.0 * jax.random.randint(sign_key, (RMAX, 1), 0, 2, jnp.int32).astype(jnp.float32)
    col_signs = 1.0 - 2.0 * jax.random.randint(turn_key, (1, RMAX), 0, 2, jnp.int32).astype(jnp.float32)
    return row_signs * col_signs * hadamard_part * small_part


def draw_u_factors(key, part):
    column_order = support_order(key)
    gain_key, noise_key, place_key = jax.random.split(jax.random.fold_in(key, 31), 3)
    gains = jax.random.uniform(gain_key, (NT, NT, RMAX, 1), jnp.float32, 1.2, 3.5)
    place_keys = jax.random.split(place_key, NT * NT)
    row_places = jax.vmap(lambda single: jax.random.permutation(single, RMAX))(place_keys).astype(jnp.int32).reshape(NT, NT, RMAX, 1)
    leading = (column_order[None, None, None, :] == row_places).astype(jnp.float32)
    noise_part = jax.random.truncated_normal(noise_key, -4.0, 4.0, (NT, NT, RMAX, B), jnp.float32)
    return (leading * gains + noise_part * (0.6 / math.sqrt(B))).astype(jnp.bfloat16)


def draw_v_factors(key, part):
    column_order = support_order(key)
    gain_key, noise_key = jax.random.split(jax.random.fold_in(key, 37))
    gains = jax.random.uniform(gain_key, (NT, NT, RMAX, 1), jnp.float32, 1.2, 3.5)
    slots = jnp.arange(RMAX, dtype=jnp.int32)
    leading = (column_order[None, :] == slots[:, None]).astype(jnp.float32)
    noise_part = jax.random.truncated_normal(noise_key, -4.0, 4.0, (NT, NT, RMAX, B), jnp.float32)
    return (leading[None, None] * gains + noise_part * (0.6 / math.sqrt(B))).astype(jnp.bfloat16)


def draw_sketch(key, part):
    column_order = support_order(key)
    table = mixing_table(key)
    gain_key, noise_key = jax.random.split(jax.random.fold_in(key, 41))
    gains = jax.random.uniform(gain_key, (RMAX, 1), jnp.float32, 0.2, 0.4)
    inside = column_order < RMAX
    picked = jnp.take(table, jnp.minimum(column_order, RMAX - 1), axis=1)
    leading = jnp.where(inside[None, :], picked, 0.0) * gains
    noise_part = jax.random.truncated_normal(noise_key, -4.0, 4.0, (RMAX, B), jnp.float32)
    return (leading + noise_part * (0.12 / math.sqrt(B))).astype(jnp.bfloat16)


def draw_diag_tiles(key, part):
    level_key, side_key, order_key, sign_key = jax.random.split(jax.random.fold_in(key, 61), 4)
    share_count = 4
    low_floor, high_floor, high_top = (2.0, 6.5, 8.0)
    high_side = jax.random.randint(side_key, (NT, B), 0, share_count, jnp.int32) == 0
    fraction = jax.random.uniform(level_key, (NT, B), jnp.float32)
    spectrum = jnp.where(high_side, high_floor + fraction * (high_top - high_floor), low_floor + fraction)
    cells = jnp.arange(B, dtype=jnp.int32)
    walsh_table = walsh_sign(cells[:, None], cells[None, :])
    profile = jnp.dot(spectrum, walsh_table, precision=lax.Precision.HIGHEST) / B
    order_keys = jax.random.split(order_key, NT)
    places = jax.vmap(lambda single: jax.random.permutation(single, B))(order_keys).astype(jnp.int32)
    signs = 1.0 - 2.0 * jax.random.randint(sign_key, (NT, B), 0, 2, jnp.int32).astype(jnp.float32)
    offsets = jnp.bitwise_xor(places[:, :, None], places[:, None, :]).reshape(NT, B * B)
    values = jnp.take_along_axis(profile, offsets, axis=1).reshape(NT, B, B)
    column_order = support_order(key)
    lifted = jnp.where(column_order < RMAX, 12.0, 0.0)
    return signs[:, :, None] * signs[:, None, :] * values + jnp.diag(lifted)[None]


def draw_rank_levels(key, part):
    level_key, row_key, col_key = jax.random.split(jax.random.fold_in(key, 17), 3)
    levels = jax.random.randint(level_key, (PANELS + 1, NT, NT), 1, 4, jnp.int32)
    levels = lax.cummin(levels, axis=0)
    big_row = jax.random.randint(row_key, (), PANELS + 1, NT, jnp.int32)
    big_col = jax.random.randint(col_key, (), PANELS, big_row, jnp.int32)
    row_groups = NT // TR
    col_groups = NT // TC
    row_slot = big_row % row_groups * TR + big_row // row_groups
    col_slot = big_col % col_groups * TC + big_col // col_groups
    levels = levels.at[:, row_slot, col_slot].set(3)
    return levels * BUCKET


def steps_of(own_key, dims, shards, least, top_value):
    def one(dim, shards_of):
        draws = jax.random.uniform(jax.random.fold_in(jax.random.fold_in(own_key, 6), dim), (shards_of,), jnp.float32, least / len(shards), top_value / len(shards))
        return jnp.repeat(jnp.exp(draws), dims[dim] // shards_of).reshape((-1,) + (1,) * (len(dims) - dim - 1))

    level = one(*shards[0])
    for cut in shards[1:]:
        level = level * one(*cut)
    return level


def setup_inputs(seed: int = 0) -> dict:
    splits = jax.random.split(jax.random.key(seed), 6)
    u_factors = draw_u_factors(jax.random.fold_in(splits[5], 71), 0)
    v_factors = draw_v_factors(jax.random.fold_in(splits[5], 71), 0)
    diag_tiles = draw_diag_tiles(jax.random.fold_in(splits[5], 71), 0)
    sketch = draw_sketch(jax.random.fold_in(splits[5], 71), 0)
    rank_levels = draw_rank_levels(jax.random.fold_in(splits[5], 71), 0)
    return dict(u_factors=u_factors, v_factors=v_factors, diag_tiles=diag_tiles, sketch=sketch, rank_levels=rank_levels)


highest = lax.Precision.HIGHEST

def product(form, left, right):
    return jnp.einsum(form, left.astype(jnp.float32), right.astype(jnp.float32), precision=highest)

def tile_of_row(position):
    return position % TR * N_ROW + position // TR

def tile_of_col(position):
    return position % TC * N_COL + position // TC

def storage_row(tile_index):
    return tile_index % N_ROW * TR + tile_index // N_ROW

def chol_apply(factor, rhs):
    middle = jax.scipy.linalg.solve_triangular(factor, rhs, lower=True)
    return jax.scipy.linalg.solve_triangular(factor, middle, lower=True, trans=1)

def solve_panel(chol_k, raw_factors):
    tile_count, rank_width, tile_order = raw_factors.shape
    flattened = raw_factors.reshape(tile_count * rank_width, tile_order).astype(jnp.float32).T
    solved = jax.scipy.linalg.solve_triangular(chol_k, flattened, lower=True)
    return solved.T.reshape(tile_count, rank_width, tile_order).astype(jnp.bfloat16)

def reference(u_factors, v_factors, diag_tiles, sketch, rank_levels):
    positions = jnp.arange(NT, dtype=jnp.int32)
    row_tile = tile_of_row(positions)
    col_tile = tile_of_col(positions)
    rank_slots = jnp.arange(RMAX, dtype=jnp.int32)
    identity = jnp.eye(RMAX, dtype=jnp.float32)
    below_diag = row_tile[:, None] > col_tile[None, :]
    live_rows = (rank_slots[None, None, :] < rank_levels[0][:, :, None]) & below_diag[:, :, None]
    zero_bf = jnp.zeros((), jnp.bfloat16)
    factor_u = jnp.where(live_rows[..., None], u_factors, zero_bf)
    factor_v = jnp.where(live_rows[..., None], v_factors, zero_bf)
    diagonal = diag_tiles
    for panel_index in range(PANELS):
        diag_pos = panel_index % N_ROW * TR + panel_index // N_ROW
        col_pos = panel_index % N_COL * TC + panel_index // N_COL
        chol_k = jnp.linalg.cholesky(diagonal[diag_pos])
        below_panel = row_tile > panel_index
        panel_u = jnp.where(below_panel[:, None, None], factor_u[:, col_pos], zero_bf)
        panel_v = jnp.where(below_panel[:, None, None], solve_panel(chol_k, factor_v[:, col_pos]), zero_bf)
        col_source = storage_row(col_tile)
        col_u = panel_u[col_source]
        col_v = panel_v[col_source]
        col_sketch = product('rx,qsx->qrs', sketch, col_u)
        new_rank = rank_levels[panel_index + 1]

        def one_row(items):
            row_u, row_v, row_diag, own_u, own_v, rank_row, tile_index = items
            coupling = product('rx,qsx->qrs', own_v, col_v)
            sketch_v = product('rx,qsx->qrs', sketch, row_v).astype(jnp.bfloat16)
            sketch_c = product('qrs,qts->qrt', col_sketch, coupling).astype(jnp.bfloat16)
            range_y = product('qrs,qsx->qrx', sketch_v, row_u) - product('qrs,sx->qrx', sketch_c, own_u)
            keep_rows = rank_slots[None, :] < rank_row[:, None]
            range_y = jnp.where(keep_rows[..., None], range_y, 0.0).astype(jnp.bfloat16)
            gram_matrix = product('qrx,qsx->qrs', range_y, range_y) + (1.0 - keep_rows.astype(jnp.float32))[:, :, None] * identity[None]
            proj_u = product('qrx,qsx->qrs', range_y, row_u)
            proj_own = product('qrx,sx->qrs', range_y, own_u)
            proj_c = product('qrs,qst->qrt', proj_own, coupling)
            gram_chol = jnp.linalg.cholesky(gram_matrix)
            first_core = chol_apply(gram_chol, proj_u).astype(jnp.bfloat16)
            second_core = chol_apply(gram_chol, proj_c).astype(jnp.bfloat16)
            fresh_v = (product('qrs,qsx->qrx', first_core, row_v) - product('qrs,qsx->qrx', second_core, col_u)).astype(jnp.bfloat16)
            update_mask = (tile_index > col_tile) & (col_tile > panel_index)
            at_panel = (col_tile == panel_index) & (tile_index > panel_index)
            new_u = jnp.where(update_mask[:, None, None], range_y, jnp.where(at_panel[:, None, None], own_u[None], row_u))
            new_v = jnp.where(update_mask[:, None, None], fresh_v, jnp.where(at_panel[:, None, None], own_v[None], row_v))
            self_c = product('rx,sx->rs', own_v, own_v).astype(jnp.bfloat16)
            spread = product('rs,sx->rx', self_c, own_u).astype(jnp.bfloat16)
            lowered = row_diag - product('rx,ry->xy', own_u, spread)
            new_diag = jnp.where(tile_index > panel_index, lowered, jnp.where(tile_index == panel_index, chol_k, row_diag))
            return (new_u, new_v, new_diag)
        factor_u, factor_v, diagonal = lax.map(one_row, (factor_u, factor_v, diagonal, panel_u, panel_v, new_rank, row_tile))
    return (factor_u, factor_v, diagonal)
```

```python
import jax
import jax.numpy as jnp
from jax import lax
from jax.sharding import PartitionSpec as P

PANELS = 2


highest = lax.Precision.HIGHEST


def broadcast(shard, axis, root):
    mine = lax.axis_index(axis) == root
    return lax.psum(jnp.where(mine, shard, jnp.zeros_like(shard)), axis)


def chol_apply(factor, rhs):
    middle = jax.scipy.linalg.solve_triangular(factor, rhs, lower=True)
    return jax.scipy.linalg.solve_triangular(factor, middle, lower=True, trans=1)


def solve_panel(chol_k, raw_factors):
    tile_count, rank_width, tile_order = raw_factors.shape
    flattened = raw_factors.reshape(tile_count * rank_width, tile_order).astype(jnp.float32).T
    solved = jax.scipy.linalg.solve_triangular(chol_k, flattened, lower=True)
    return solved.T.reshape(tile_count, rank_width, tile_order).astype(jnp.bfloat16)


def factor_tile(tile_mat):
    return jnp.linalg.cholesky(tile_mat)


def zero_tile(tile_mat):
    return jnp.zeros_like(tile_mat)


def zero_factors(chol_k, raw_factors):
    return jnp.zeros_like(raw_factors)


def on_device(u_factors, v_factors, diag_tiles, sketch, rank_levels):
    row_count = lax.axis_size("row")
    col_count = lax.axis_size("col")
    row_index = lax.axis_index("row")
    col_index = lax.axis_index("col")
    tiles_row, tiles_col, rank_width, tile_order = u_factors.shape
    diag_rows = diag_tiles.shape[1]
    col_ratio = col_count // row_count
    row_tile = jnp.arange(tiles_row, dtype=jnp.int32) * row_count + row_index
    col_tile = jnp.arange(tiles_col, dtype=jnp.int32) * col_count + col_index
    rank_slots = jnp.arange(rank_width, dtype=jnp.int32)
    identity = jnp.eye(rank_width, dtype=jnp.float32)
    zero_bf = jnp.zeros((), jnp.bfloat16)
    below_diag = row_tile[:, None] > col_tile[None, :]
    live_rows = (rank_slots[None, None, :] < rank_levels[0][:, :, None]) & below_diag[:, :, None]
    factor_u = jnp.where(live_rows[..., None], u_factors, zero_bf)
    factor_v = jnp.where(live_rows[..., None], v_factors, zero_bf)
    diagonal = diag_tiles
    first_row = col_index * diag_rows
    pick_slot = col_index // row_count
    for panel_index in range(PANELS):
        diag_slot = panel_index // row_count
        diag_owner = panel_index % row_count
        col_slot = panel_index // col_count
        col_owner = panel_index % col_count
        raw_u = factor_u[:, col_slot]
        raw_v = factor_v[:, col_slot]
        row_u, row_raw = (
            broadcast(raw_u, "col", col_owner),
            broadcast(raw_v, "col", col_owner),
        )
        relay_u = lax.dynamic_index_in_dim(
            row_u.reshape(tiles_col, col_ratio, rank_width, tile_order),
            pick_slot,
            1,
            keepdims=False,
        )
        relay_v = lax.dynamic_index_in_dim(
            row_raw.reshape(tiles_col, col_ratio, rank_width, tile_order),
            pick_slot,
            1,
            keepdims=False,
        )
        col_u, col_raw = (
            broadcast(relay_u, "row", col_index % row_count),
            broadcast(relay_v, "row", col_index % row_count),
        )
        whole_tile = lax.all_gather(diagonal[diag_slot], "col", axis=0, tiled=True)
        own_chol = lax.cond(row_index == diag_owner, factor_tile, zero_tile, whole_tile)
        chol_k = broadcast(own_chol, "row", diag_owner)
        solved = solve_panel(chol_k, jnp.concatenate([row_raw, col_raw], axis=0))
        row_v = solved[:tiles_row]
        col_v = solved[tiles_row:]
        row_live = (row_tile > panel_index)[:, None, None]
        col_live = (col_tile > panel_index)[:, None, None]
        row_u = jnp.where(row_live, row_u, zero_bf)
        row_v = jnp.where(row_live, row_v, zero_bf)
        col_u = jnp.where(col_live, col_u, zero_bf)
        col_v = jnp.where(col_live, col_v, zero_bf)
        coupling = jnp.einsum("arx,bsx->abrs", row_v, col_v, preferred_element_type=jnp.float32)
        col_sketch = jnp.einsum("rx,bsx->brs", sketch, col_u, preferred_element_type=jnp.float32)
        sketch_v = jnp.einsum(
            "rx,absx->abrs", sketch, factor_v, preferred_element_type=jnp.float32
        ).astype(jnp.bfloat16)
        sketch_c = jnp.einsum("brs,abts->abrt", col_sketch, coupling, precision=highest).astype(
            jnp.bfloat16
        )
        range_y = jnp.einsum(
            "abrs,absx->abrx", sketch_v, factor_u, preferred_element_type=jnp.float32
        )
        range_y = range_y - jnp.einsum(
            "abrs,asx->abrx", sketch_c, row_u, preferred_element_type=jnp.float32
        )
        keep_rows = rank_slots[None, None, :] < rank_levels[panel_index + 1][:, :, None]
        range_y = jnp.where(keep_rows[..., None], range_y, 0.0).astype(jnp.bfloat16)
        gram_matrix = jnp.einsum(
            "abrx,absx->abrs", range_y, range_y, preferred_element_type=jnp.float32
        )
        gram_matrix = gram_matrix + (1.0 - keep_rows.astype(jnp.float32))[..., None] * identity
        proj_u = jnp.einsum(
            "abrx,absx->abrs", range_y, factor_u, preferred_element_type=jnp.float32
        )
        proj_own = jnp.einsum("abrx,asx->abrs", range_y, row_u, preferred_element_type=jnp.float32)
        proj_c = jnp.einsum("abrs,abst->abrt", proj_own, coupling, precision=highest)
        gram_chol = jnp.linalg.cholesky(gram_matrix)
        gram_inv = jax.scipy.linalg.solve_triangular(
            gram_chol, jnp.broadcast_to(identity, gram_chol.shape), lower=True
        )
        both = jnp.concatenate([proj_u, proj_c], axis=-1)
        middle = jnp.einsum("abrs,abst->abrt", gram_inv, both, precision=highest)
        cores = jnp.einsum("absr,abst->abrt", gram_inv, middle, precision=highest)
        first_core = cores[..., :rank_width].astype(jnp.bfloat16)
        second_core = cores[..., rank_width:].astype(jnp.bfloat16)
        fresh_v = jnp.einsum(
            "abrs,absx->abrx", first_core, factor_v, preferred_element_type=jnp.float32
        )
        fresh_v = (
            fresh_v
            - jnp.einsum("abrs,bsx->abrx", second_core, col_u, preferred_element_type=jnp.float32)
        ).astype(jnp.bfloat16)
        update_mask = ((row_tile[:, None] > col_tile[None, :]) & (col_tile[None, :] > panel_index))[
            ..., None, None
        ]
        at_panel = ((col_tile[None, :] == panel_index) & (row_tile[:, None] > panel_index))[
            ..., None, None
        ]
        factor_u = jnp.where(update_mask, range_y, jnp.where(at_panel, row_u[:, None], factor_u))
        factor_v = jnp.where(update_mask, fresh_v, jnp.where(at_panel, row_v[:, None], factor_v))
        self_c = jnp.einsum(
            "arx,asx->ars", row_v, row_v, preferred_element_type=jnp.float32
        ).astype(jnp.bfloat16)
        spread = jnp.einsum(
            "ars,asx->arx", self_c, row_u, preferred_element_type=jnp.float32
        ).astype(jnp.bfloat16)
        part_u = lax.dynamic_slice_in_dim(row_u, first_row, diag_rows, 2)
        lowered = diagonal - jnp.einsum(
            "arx,ary->axy", part_u, spread, preferred_element_type=jnp.float32
        )
        chol_rows = lax.dynamic_slice_in_dim(chol_k, first_row, diag_rows, 0)
        diag_tile = row_tile[:, None, None]
        diagonal = jnp.where(
            diag_tile > panel_index,
            lowered,
            jnp.where(diag_tile == panel_index, chol_rows[None], diagonal),
        )
    return (factor_u, factor_v, diagonal)


def solution(mesh):
    in_specs = (
        P("row", "col", None, None),
        P("row", "col", None, None),
        P("row", "col", None),
        P(),
        P(None, "row", "col"),
    )
    out_specs = (P("row", "col", None, None), P("row", "col", None, None), P("row", "col", None))
    return jax.shard_map(
        on_device, mesh=mesh, in_specs=in_specs, out_specs=out_specs, check_vma=False
    )
```

```python
import jax
import jax.numpy as jnp
from jax import lax
from jax.sharding import PartitionSpec as P

PANELS = 2


highest = lax.Precision.HIGHEST


def broadcast(shard, axis, root):
    mine = lax.axis_index(axis) == root
    return lax.psum(jnp.where(mine, shard, jnp.zeros_like(shard)), axis)


def chol_apply(factor, rhs):
    middle = jax.scipy.linalg.solve_triangular(factor, rhs, lower=True)
    return jax.scipy.linalg.solve_triangular(factor, middle, lower=True, trans=1)


def solve_panel(chol_k, raw_factors):
    tile_count, rank_width, tile_order = raw_factors.shape
    flattened = raw_factors.reshape(tile_count * rank_width, tile_order).astype(jnp.float32).T
    solved = jax.scipy.linalg.solve_triangular(chol_k, flattened, lower=True)
    return solved.T.reshape(tile_count, rank_width, tile_order).astype(jnp.bfloat16)


BLOCK = 128


def factor_tile(tile_mat):
    order = tile_mat.shape[0]
    width = min(BLOCK, order)
    count = order // width
    work = (tile_mat + tile_mat.T) * 0.5
    eye = jnp.eye(width, dtype=jnp.float32)
    strips = []
    for step in range(count):
        head = jnp.tril(lax.linalg.cholesky(work[:width, :width], symmetrize_input=False))
        head_inv = lax.linalg.triangular_solve(head, eye, left_side=True, lower=True)
        parts = [jnp.zeros((step * width, width), jnp.float32), head + jnp.triu(head_inv.T, 1)]
        if step < count - 1:
            below = jnp.dot(work[width:, :width], head_inv.T, precision=highest)
            work = work[width:, width:] - jnp.dot(below, below.T, precision=highest)
            parts.append(below)
        strips.append(jnp.concatenate(parts, axis=0))
    return jnp.concatenate(strips, axis=1)


def solve_packed(packed, raw_factors):
    order = packed.shape[0]
    width = min(BLOCK, order)
    count = order // width
    lead = raw_factors.shape[:-1]
    rows = raw_factors.reshape(-1, order).astype(jnp.float32)
    done = []
    for step in range(count):
        lo, hi = step * width, (step + 1) * width
        block = packed[lo:hi, lo:hi]
        inverse = jnp.tril(block.T, -1) + jnp.diag(1.0 / jnp.diagonal(block))
        rhs = rows[:, lo:hi]
        if step:
            prior = jnp.concatenate(done, axis=1)
            rhs = rhs - jnp.dot(prior, packed[lo:hi, :lo].T, precision=highest)
        done.append(jnp.dot(rhs, inverse.T, precision=highest))
    return jnp.concatenate(done, axis=1).reshape(lead + (order,)).astype(jnp.bfloat16)


def zero_tile(tile_mat):
    return jnp.zeros_like(tile_mat)


def zero_factors(chol_k, raw_factors):
    return jnp.zeros_like(raw_factors)


def on_device(u_factors, v_factors, diag_tiles, sketch, rank_levels):
    row_count = lax.axis_size("row")
    col_count = lax.axis_size("col")
    row_index = lax.axis_index("row")
    col_index = lax.axis_index("col")
    tiles_row, tiles_col, rank_width, tile_order = u_factors.shape
    diag_rows = diag_tiles.shape[1]
    col_ratio = col_count // row_count
    row_tile = jnp.arange(tiles_row, dtype=jnp.int32) * row_count + row_index
    col_tile = jnp.arange(tiles_col, dtype=jnp.int32) * col_count + col_index
    rank_slots = jnp.arange(rank_width, dtype=jnp.int32)
    identity = jnp.eye(rank_width, dtype=jnp.float32)
    zero_bf = jnp.zeros((), jnp.bfloat16)
    below_diag = row_tile[:, None] > col_tile[None, :]
    live_rows = (rank_slots[None, None, :] < rank_levels[0][:, :, None]) & below_diag[:, :, None]
    factor_u = jnp.where(live_rows[..., None], u_factors, zero_bf)
    factor_v = jnp.where(live_rows[..., None], v_factors, zero_bf)
    diagonal = diag_tiles
    first_row = col_index * diag_rows
    pick_slot = col_index // row_count
    chol_cols = jnp.arange(tile_order, dtype=jnp.int32)[None, :]
    chol_rows_at = first_row + jnp.arange(diag_rows, dtype=jnp.int32)[:, None]
    whole_tile = None
    for panel_index in range(PANELS):
        diag_slot = panel_index // row_count
        diag_owner = panel_index % row_count
        col_slot = panel_index // col_count
        col_owner = panel_index % col_count
        raw_u = factor_u[:, col_slot]
        raw_v = factor_v[:, col_slot]
        if whole_tile is None:
            whole_tile = lax.all_gather(diagonal[diag_slot], "col", axis=0, tiled=True)
            whole_tile, raw_u, raw_v = lax.optimization_barrier((whole_tile, raw_u, raw_v))
        row_u, row_raw = (
            broadcast(raw_u, "col", col_owner),
            broadcast(raw_v, "col", col_owner),
        )
        relay_u = lax.dynamic_index_in_dim(
            row_u.reshape(tiles_col, col_ratio, rank_width, tile_order),
            pick_slot,
            1,
            keepdims=False,
        )
        relay_v = lax.dynamic_index_in_dim(
            row_raw.reshape(tiles_col, col_ratio, rank_width, tile_order),
            pick_slot,
            1,
            keepdims=False,
        )
        col_u, col_raw = (
            broadcast(relay_u, "row", col_index % row_count),
            broadcast(relay_v, "row", col_index % row_count),
        )
        own_chol = lax.cond(row_index == diag_owner, factor_tile, zero_tile, whole_tile)
        whole_tile = None
        chol_k = broadcast(own_chol, "row", diag_owner)
        solved = solve_packed(chol_k, jnp.concatenate([row_raw, col_raw], axis=0))
        row_v = solved[:tiles_row]
        col_v = solved[tiles_row:]
        row_live = (row_tile > panel_index)[:, None, None]
        col_live = (col_tile > panel_index)[:, None, None]
        row_u = jnp.where(row_live, row_u, zero_bf)
        row_v = jnp.where(row_live, row_v, zero_bf)
        col_u = jnp.where(col_live, col_u, zero_bf)
        col_v = jnp.where(col_live, col_v, zero_bf)
        self_c = jnp.einsum(
            "arx,asx->ars", row_v, row_v, preferred_element_type=jnp.float32
        ).astype(jnp.bfloat16)
        spread = jnp.einsum(
            "ars,asx->arx", self_c, row_u, preferred_element_type=jnp.float32
        ).astype(jnp.bfloat16)
        part_u = lax.dynamic_slice_in_dim(row_u, first_row, diag_rows, 2)
        lowered = diagonal - jnp.einsum(
            "arx,ary->axy", part_u, spread, preferred_element_type=jnp.float32
        )
        chol_rows = lax.dynamic_slice_in_dim(chol_k, first_row, diag_rows, 0)
        chol_rows = jnp.where(chol_cols <= chol_rows_at, chol_rows, 0.0)
        diag_tile = row_tile[:, None, None]
        diagonal = jnp.where(
            diag_tile > panel_index,
            lowered,
            jnp.where(diag_tile == panel_index, chol_rows[None], diagonal),
        )
        if panel_index + 1 < PANELS:
            next_slot = (panel_index + 1) // row_count
            whole_tile = lax.all_gather(diagonal[next_slot], "col", axis=0, tiled=True)
        coupling = jnp.einsum("arx,bsx->abrs", row_v, col_v, preferred_element_type=jnp.float32)
        col_sketch = jnp.einsum("rx,bsx->brs", sketch, col_u, preferred_element_type=jnp.float32)
        sketch_v = jnp.einsum(
            "rx,absx->abrs", sketch, factor_v, preferred_element_type=jnp.float32
        ).astype(jnp.bfloat16)
        sketch_c = jnp.einsum("brs,abts->abrt", col_sketch, coupling, precision=highest).astype(
            jnp.bfloat16
        )
        range_y = jnp.einsum(
            "abrs,absx->abrx", sketch_v, factor_u, preferred_element_type=jnp.float32
        )
        range_y = range_y - jnp.einsum(
            "abrs,asx->abrx", sketch_c, row_u, preferred_element_type=jnp.float32
        )
        keep_rows = rank_slots[None, None, :] < rank_levels[panel_index + 1][:, :, None]
        range_y = jnp.where(keep_rows[..., None], range_y, 0.0).astype(jnp.bfloat16)
        gram_matrix = jnp.einsum(
            "abrx,absx->abrs", range_y, range_y, preferred_element_type=jnp.float32
        )
        gram_matrix = gram_matrix + (1.0 - keep_rows.astype(jnp.float32))[..., None] * identity
        if whole_tile is not None:
            whole_tile, gram_matrix = lax.optimization_barrier((whole_tile, gram_matrix))
        proj_u = jnp.einsum(
            "abrx,absx->abrs", range_y, factor_u, preferred_element_type=jnp.float32
        )
        proj_own = jnp.einsum("abrx,asx->abrs", range_y, row_u, preferred_element_type=jnp.float32)
        proj_c = jnp.einsum("abrs,abst->abrt", proj_own, coupling, precision=highest)
        gram_chol = jnp.linalg.cholesky(gram_matrix)
        gram_inv = jax.scipy.linalg.solve_triangular(
            gram_chol, jnp.broadcast_to(identity, gram_chol.shape), lower=True
        )
        both = jnp.concatenate([proj_u, proj_c], axis=-1)
        middle = jnp.einsum("abrs,abst->abrt", gram_inv, both, precision=highest)
        cores = jnp.einsum("absr,abst->abrt", gram_inv, middle, precision=highest)
        first_core = cores[..., :rank_width].astype(jnp.bfloat16)
        second_core = cores[..., rank_width:].astype(jnp.bfloat16)
        fresh_v = jnp.einsum(
            "abrs,absx->abrx", first_core, factor_v, preferred_element_type=jnp.float32
        )
        fresh_v = (
            fresh_v
            - jnp.einsum("abrs,bsx->abrx", second_core, col_u, preferred_element_type=jnp.float32)
        ).astype(jnp.bfloat16)
        if whole_tile is not None:
            whole_tile, fresh_v = lax.optimization_barrier((whole_tile, fresh_v))
        update_mask = ((row_tile[:, None] > col_tile[None, :]) & (col_tile[None, :] > panel_index))[
            ..., None, None
        ]
        at_panel = ((col_tile[None, :] == panel_index) & (row_tile[:, None] > panel_index))[
            ..., None, None
        ]
        factor_u = jnp.where(update_mask, range_y, jnp.where(at_panel, row_u[:, None], factor_u))
        factor_v = jnp.where(update_mask, fresh_v, jnp.where(at_panel, row_v[:, None], factor_v))
    return (factor_u, factor_v, diagonal)


def solution(mesh):
    in_specs = (
        P("row", "col", None, None),
        P("row", "col", None, None),
        P("row", "col", None),
        P(),
        P(None, "row", "col"),
    )
    out_specs = (P("row", "col", None, None), P("row", "col", None, None), P("row", "col", None))
    return jax.shard_map(
        on_device, mesh=mesh, in_specs=in_specs, out_specs=out_specs, check_vma=False
    )
```

```python
import jax
import jax.numpy as jnp
from jax import lax
from jax.sharding import PartitionSpec as P

PANELS = 2


highest = lax.Precision.HIGHEST


def broadcast(shard, axis, root):
    mine = lax.axis_index(axis) == root
    return lax.psum(jnp.where(mine, shard, jnp.zeros_like(shard)), axis)


def chol_apply(factor, rhs):
    middle = jax.scipy.linalg.solve_triangular(factor, rhs, lower=True)
    return jax.scipy.linalg.solve_triangular(factor, middle, lower=True, trans=1)


def solve_panel(chol_k, raw_factors):
    tile_count, rank_width, tile_order = raw_factors.shape
    flattened = raw_factors.reshape(tile_count * rank_width, tile_order).astype(jnp.float32).T
    solved = jax.scipy.linalg.solve_triangular(chol_k, flattened, lower=True)
    return solved.T.reshape(tile_count, rank_width, tile_order).astype(jnp.bfloat16)


BLOCK = 128


def factor_tile(tile_mat):
    order = tile_mat.shape[0]
    width = min(BLOCK, order)
    count = order // width
    work = (tile_mat + tile_mat.T) * 0.5
    eye = jnp.eye(width, dtype=jnp.float32)
    strips = []
    for step in range(count):
        head = jnp.tril(lax.linalg.cholesky(work[:width, :width], symmetrize_input=False))
        head_inv = lax.linalg.triangular_solve(head, eye, left_side=True, lower=True)
        parts = [jnp.zeros((step * width, width), jnp.float32), head + jnp.triu(head_inv.T, 1)]
        if step < count - 1:
            below = jnp.dot(work[width:, :width], head_inv.T, precision=highest)
            work = work[width:, width:] - jnp.dot(below, below.T, precision=highest)
            parts.append(below)
        strips.append(jnp.concatenate(parts, axis=0))
    return jnp.concatenate(strips, axis=1)


def factor_inverse(gram):
    order = gram.shape[-1]
    width = min(BLOCK, order)
    gram = (gram + jnp.swapaxes(gram, -1, -2)) * 0.5
    eye = jnp.broadcast_to(jnp.eye(width, dtype=jnp.float32), gram.shape[:-2] + (width, width))
    head = jnp.tril(lax.linalg.cholesky(gram[..., :width, :width], symmetrize_input=False))
    head_inv = lax.linalg.triangular_solve(head, eye, left_side=True, lower=True)
    if width == order:
        return head_inv
    rest = order - width
    below = jnp.einsum("...ij,...kj->...ik", gram[..., width:, :width], head_inv, precision=highest)
    tail = gram[..., width:, width:] - jnp.einsum("...ij,...kj->...ik", below, below, precision=highest)
    tail = jnp.tril(lax.linalg.cholesky(tail, symmetrize_input=False))
    eye_rest = jnp.broadcast_to(jnp.eye(rest, dtype=jnp.float32), gram.shape[:-2] + (rest, rest))
    tail_inv = lax.linalg.triangular_solve(tail, eye_rest, left_side=True, lower=True)
    cross = jnp.einsum("...ij,...jk->...ik", below, head_inv, precision=highest)
    cross = -jnp.einsum("...ij,...jk->...ik", tail_inv, cross, precision=highest)
    top = jnp.concatenate([head_inv, jnp.zeros(gram.shape[:-2] + (width, rest), jnp.float32)], -1)
    return jnp.concatenate([top, jnp.concatenate([cross, tail_inv], -1)], -2)


def solve_packed(packed, raw_factors):
    order = packed.shape[0]
    width = min(BLOCK, order)
    count = order // width
    lead = raw_factors.shape[:-1]
    rows = raw_factors.reshape(-1, order).astype(jnp.float32)
    done = []
    for step in range(count):
        lo, hi = step * width, (step + 1) * width
        block = packed[lo:hi, lo:hi]
        inverse = jnp.tril(block.T, -1) + jnp.diag(1.0 / jnp.diagonal(block))
        rhs = rows[:, lo:hi]
        if step:
            prior = jnp.concatenate(done, axis=1)
            rhs = rhs - jnp.dot(prior, packed[lo:hi, :lo].T, precision=highest)
        done.append(jnp.dot(rhs, inverse.T, precision=highest))
    return jnp.concatenate(done, axis=1).reshape(lead + (order,)).astype(jnp.bfloat16)


def zero_tile(tile_mat):
    return jnp.zeros_like(tile_mat)


def zero_factors(chol_k, raw_factors):
    return jnp.zeros_like(raw_factors)


def on_device(u_factors, v_factors, diag_tiles, sketch, rank_levels):
    row_count = lax.axis_size("row")
    col_count = lax.axis_size("col")
    row_index = lax.axis_index("row")
    col_index = lax.axis_index("col")
    tiles_row, tiles_col, rank_width, tile_order = u_factors.shape
    diag_rows = diag_tiles.shape[1]
    col_ratio = col_count // row_count
    row_tile = jnp.arange(tiles_row, dtype=jnp.int32) * row_count + row_index
    col_tile = jnp.arange(tiles_col, dtype=jnp.int32) * col_count + col_index
    rank_slots = jnp.arange(rank_width, dtype=jnp.int32)
    identity = jnp.eye(rank_width, dtype=jnp.float32)
    zero_bf = jnp.zeros((), jnp.bfloat16)
    below_diag = row_tile[:, None] > col_tile[None, :]
    live_rows = (rank_slots[None, None, :] < rank_levels[0][:, :, None]) & below_diag[:, :, None]
    factor_u = jnp.where(live_rows[..., None], u_factors, zero_bf)
    factor_v = jnp.where(live_rows[..., None], v_factors, zero_bf)
    diagonal = diag_tiles
    first_row = col_index * diag_rows
    pick_slot = col_index // row_count
    chol_cols = jnp.arange(tile_order, dtype=jnp.int32)[None, :]
    chol_rows_at = first_row + jnp.arange(diag_rows, dtype=jnp.int32)[:, None]
    whole_tile = None
    for panel_index in range(PANELS):
        diag_slot = panel_index // row_count
        diag_owner = panel_index % row_count
        col_slot = panel_index // col_count
        col_owner = panel_index % col_count
        raw_u = factor_u[:, col_slot]
        raw_v = factor_v[:, col_slot]
        if whole_tile is None:
            whole_tile = lax.all_gather(diagonal[diag_slot], "col", axis=0, tiled=True)
            whole_tile, raw_u, raw_v = lax.optimization_barrier((whole_tile, raw_u, raw_v))
        row_u, row_raw = (
            broadcast(raw_u, "col", col_owner),
            broadcast(raw_v, "col", col_owner),
        )
        relay_u = lax.dynamic_index_in_dim(
            row_u.reshape(tiles_col, col_ratio, rank_width, tile_order),
            pick_slot,
            1,
            keepdims=False,
        )
        relay_v = lax.dynamic_index_in_dim(
            row_raw.reshape(tiles_col, col_ratio, rank_width, tile_order),
            pick_slot,
            1,
            keepdims=False,
        )
        own_chol = lax.cond(row_index == diag_owner, factor_tile, zero_tile, whole_tile)
        whole_tile = None
        relay_here = row_index == col_index % row_count
        relay = jnp.concatenate([relay_u, relay_v], axis=0).astype(jnp.float32)
        relay = jnp.where(relay_here, relay, jnp.zeros_like(relay))
        own_chol = jnp.where(row_index == diag_owner, own_chol, jnp.zeros_like(own_chol))
        merged = lax.psum(
            jnp.concatenate([own_chol, relay.reshape(-1, tile_order)], axis=0), "row"
        )
        chol_k = merged[:tile_order]
        relay = merged[tile_order:].reshape(relay.shape).astype(jnp.bfloat16)
        col_u = relay[:tiles_col]
        col_raw = relay[tiles_col:]
        solved = solve_packed(chol_k, jnp.concatenate([row_raw, col_raw], axis=0))
        row_v = solved[:tiles_row]
        col_v = solved[tiles_row:]
        row_live = (row_tile > panel_index)[:, None, None]
        col_live = (col_tile > panel_index)[:, None, None]
        row_u = jnp.where(row_live, row_u, zero_bf)
        row_v = jnp.where(row_live, row_v, zero_bf)
        col_u = jnp.where(col_live, col_u, zero_bf)
        col_v = jnp.where(col_live, col_v, zero_bf)
        self_c = jnp.einsum(
            "arx,asx->ars", row_v, row_v, preferred_element_type=jnp.float32
        ).astype(jnp.bfloat16)
        spread = jnp.einsum(
            "ars,asx->arx", self_c, row_u, preferred_element_type=jnp.float32
        ).astype(jnp.bfloat16)
        part_u = lax.dynamic_slice_in_dim(row_u, first_row, diag_rows, 2)
        lowered = diagonal - jnp.einsum(
            "arx,ary->axy", part_u, spread, preferred_element_type=jnp.float32
        )
        chol_rows = lax.dynamic_slice_in_dim(chol_k, first_row, diag_rows, 0)
        chol_rows = jnp.where(chol_cols <= chol_rows_at, chol_rows, 0.0)
        diag_tile = row_tile[:, None, None]
        diagonal = jnp.where(
            diag_tile > panel_index,
            lowered,
            jnp.where(diag_tile == panel_index, chol_rows[None], diagonal),
        )
        if panel_index + 1 < PANELS:
            next_slot = (panel_index + 1) // row_count
            whole_tile = lax.all_gather(diagonal[next_slot], "col", axis=0, tiled=True)
        coupling = jnp.einsum("arx,bsx->abrs", row_v, col_v, preferred_element_type=jnp.float32)
        col_sketch = jnp.einsum("rx,bsx->brs", sketch, col_u, preferred_element_type=jnp.float32)
        sketch_v = jnp.einsum(
            "rx,absx->abrs", sketch, factor_v, preferred_element_type=jnp.float32
        ).astype(jnp.bfloat16)
        sketch_c = jnp.einsum("brs,abts->abrt", col_sketch, coupling, precision=highest).astype(
            jnp.bfloat16
        )
        range_y = jnp.einsum(
            "abrs,absx->abrx", sketch_v, factor_u, preferred_element_type=jnp.float32
        )
        range_y = range_y - jnp.einsum(
            "abrs,asx->abrx", sketch_c, row_u, preferred_element_type=jnp.float32
        )
        keep_rows = rank_slots[None, None, :] < rank_levels[panel_index + 1][:, :, None]
        range_y = jnp.where(keep_rows[..., None], range_y, 0.0).astype(jnp.bfloat16)
        gram_matrix = jnp.einsum(
            "abrx,absx->abrs", range_y, range_y, preferred_element_type=jnp.float32
        )
        gram_matrix = gram_matrix + (1.0 - keep_rows.astype(jnp.float32))[..., None] * identity
        proj_u = jnp.einsum(
            "abrx,absx->abrs", range_y, factor_u, preferred_element_type=jnp.float32
        )
        proj_own = jnp.einsum("abrx,asx->abrs", range_y, row_u, preferred_element_type=jnp.float32)
        proj_c = jnp.einsum("abrs,abst->abrt", proj_own, coupling, precision=highest)
        gram_inv = factor_inverse(gram_matrix)
        both = jnp.concatenate([proj_u, proj_c], axis=-1)
        middle = jnp.einsum("abrs,abst->abrt", gram_inv, both, precision=highest)
        cores = jnp.einsum("absr,abst->abrt", gram_inv, middle, precision=highest)
        first_core = cores[..., :rank_width].astype(jnp.bfloat16)
        second_core = cores[..., rank_width:].astype(jnp.bfloat16)
        fresh_v = jnp.einsum(
            "abrs,absx->abrx", first_core, factor_v, preferred_element_type=jnp.float32
        )
        fresh_v = (
            fresh_v
            - jnp.einsum("abrs,bsx->abrx", second_core, col_u, preferred_element_type=jnp.float32)
        ).astype(jnp.bfloat16)
        if whole_tile is not None:
            whole_tile, fresh_v = lax.optimization_barrier((whole_tile, fresh_v))
        update_mask = ((row_tile[:, None] > col_tile[None, :]) & (col_tile[None, :] > panel_index))[
            ..., None, None
        ]
        at_panel = ((col_tile[None, :] == panel_index) & (row_tile[:, None] > panel_index))[
            ..., None, None
        ]
        factor_u = jnp.where(update_mask, range_y, jnp.where(at_panel, row_u[:, None], factor_u))
        factor_v = jnp.where(update_mask, fresh_v, jnp.where(at_panel, row_v[:, None], factor_v))
    return (factor_u, factor_v, diagonal)


def solution(mesh):
    in_specs = (
        P("row", "col", None, None),
        P("row", "col", None, None),
        P("row", "col", None),
        P(),
        P(None, "row", "col"),
    )
    out_specs = (P("row", "col", None, None), P("row", "col", None, None), P("row", "col", None))
    return jax.shard_map(
        on_device, mesh=mesh, in_specs=in_specs, out_specs=out_specs, check_vma=False
    )
```

```python
import jax
import jax.numpy as jnp
from jax import lax
from jax.sharding import PartitionSpec as P

PANELS = 2


highest = lax.Precision.HIGHEST
fine = lax.Precision.HIGH


def broadcast(shard, axis, root):
    mine = lax.axis_index(axis) == root
    return lax.psum(jnp.where(mine, shard, jnp.zeros_like(shard)), axis)


def chol_apply(factor, rhs):
    middle = jax.scipy.linalg.solve_triangular(factor, rhs, lower=True)
    return jax.scipy.linalg.solve_triangular(factor, middle, lower=True, trans=1)


def solve_panel(chol_k, raw_factors):
    tile_count, rank_width, tile_order = raw_factors.shape
    flattened = raw_factors.reshape(tile_count * rank_width, tile_order).astype(jnp.float32).T
    solved = jax.scipy.linalg.solve_triangular(chol_k, flattened, lower=True)
    return solved.T.reshape(tile_count, rank_width, tile_order).astype(jnp.bfloat16)


BLOCK = 128


def factor_tile(tile_mat):
    order = tile_mat.shape[0]
    width = min(BLOCK, order)
    count = order // width
    work = (tile_mat + tile_mat.T) * 0.5
    eye = jnp.eye(width, dtype=jnp.float32)
    strips = []
    for step in range(count):
        head = jnp.tril(lax.linalg.cholesky(work[:width, :width], symmetrize_input=False))
        head_inv = lax.linalg.triangular_solve(head, eye, left_side=True, lower=True)
        parts = [jnp.zeros((step * width, width), jnp.float32), head + jnp.triu(head_inv.T, 1)]
        if step < count - 1:
            below = jnp.dot(work[width:, :width], head_inv.T, precision=fine)
            work = work[width:, width:] - jnp.dot(below, below.T, precision=fine)
            parts.append(below)
        strips.append(jnp.concatenate(parts, axis=0))
    return jnp.concatenate(strips, axis=1)


def factor_inverse(gram):
    order = gram.shape[-1]
    width = min(BLOCK, order)
    gram = (gram + jnp.swapaxes(gram, -1, -2)) * 0.5
    eye = jnp.broadcast_to(jnp.eye(width, dtype=jnp.float32), gram.shape[:-2] + (width, width))
    head = jnp.tril(lax.linalg.cholesky(gram[..., :width, :width], symmetrize_input=False))
    head_inv = lax.linalg.triangular_solve(head, eye, left_side=True, lower=True)
    if width == order:
        return head_inv
    rest = order - width
    below = jnp.einsum("...ij,...kj->...ik", gram[..., width:, :width], head_inv, precision=highest)
    tail = gram[..., width:, width:] - jnp.einsum("...ij,...kj->...ik", below, below, precision=highest)
    tail = jnp.tril(lax.linalg.cholesky(tail, symmetrize_input=False))
    eye_rest = jnp.broadcast_to(jnp.eye(rest, dtype=jnp.float32), gram.shape[:-2] + (rest, rest))
    tail_inv = lax.linalg.triangular_solve(tail, eye_rest, left_side=True, lower=True)
    cross = jnp.einsum("...ij,...jk->...ik", below, head_inv, precision=highest)
    cross = -jnp.einsum("...ij,...jk->...ik", tail_inv, cross, precision=highest)
    top = jnp.concatenate([head_inv, jnp.zeros(gram.shape[:-2] + (width, rest), jnp.float32)], -1)
    return jnp.concatenate([top, jnp.concatenate([cross, tail_inv], -1)], -2)


def solve_packed(packed, raw_factors):
    order = packed.shape[0]
    width = min(BLOCK, order)
    count = order // width
    lead = raw_factors.shape[:-1]
    rows = raw_factors.reshape(-1, order).astype(jnp.float32)
    done = []
    for step in range(count):
        lo, hi = step * width, (step + 1) * width
        block = packed[lo:hi, lo:hi]
        inverse = jnp.tril(block.T, -1) + jnp.diag(1.0 / jnp.diagonal(block))
        rhs = rows[:, lo:hi]
        if step:
            prior = jnp.concatenate(done, axis=1)
            rhs = rhs - jnp.dot(prior, packed[lo:hi, :lo].T, precision=fine)
        done.append(jnp.dot(rhs, inverse.T, precision=fine))
    return jnp.concatenate(done, axis=1).reshape(lead + (order,)).astype(jnp.bfloat16)


def zero_tile(tile_mat):
    return jnp.zeros_like(tile_mat)


def zero_factors(chol_k, raw_factors):
    return jnp.zeros_like(raw_factors)


def on_device(u_factors, v_factors, diag_tiles, sketch, rank_levels):
    row_count = lax.axis_size("row")
    col_count = lax.axis_size("col")
    row_index = lax.axis_index("row")
    col_index = lax.axis_index("col")
    tiles_row, tiles_col, rank_width, tile_order = u_factors.shape
    diag_rows = diag_tiles.shape[1]
    col_ratio = col_count // row_count
    row_tile = jnp.arange(tiles_row, dtype=jnp.int32) * row_count + row_index
    col_tile = jnp.arange(tiles_col, dtype=jnp.int32) * col_count + col_index
    rank_slots = jnp.arange(rank_width, dtype=jnp.int32)
    identity = jnp.eye(rank_width, dtype=jnp.float32)
    zero_bf = jnp.zeros((), jnp.bfloat16)
    below_diag = row_tile[:, None] > col_tile[None, :]
    live_rows = (rank_slots[None, None, :] < rank_levels[0][:, :, None]) & below_diag[:, :, None]
    factor_u = jnp.where(live_rows[..., None], u_factors, zero_bf)
    factor_v = jnp.where(live_rows[..., None], v_factors, zero_bf)
    diagonal = diag_tiles
    first_row = col_index * diag_rows
    pick_slot = col_index // row_count
    chol_cols = jnp.arange(tile_order, dtype=jnp.int32)[None, :]
    chol_rows_at = first_row + jnp.arange(diag_rows, dtype=jnp.int32)[:, None]
    whole_tile = None
    for panel_index in range(PANELS):
        diag_slot = panel_index // row_count
        diag_owner = panel_index % row_count
        col_slot = panel_index // col_count
        col_owner = panel_index % col_count
        raw_u = factor_u[:, col_slot]
        raw_v = factor_v[:, col_slot]
        if whole_tile is None:
            whole_tile = lax.all_gather(diagonal[diag_slot], "col", axis=0, tiled=True)
            whole_tile, raw_u, raw_v = lax.optimization_barrier((whole_tile, raw_u, raw_v))
        row_u, row_raw = (
            broadcast(raw_u, "col", col_owner),
            broadcast(raw_v, "col", col_owner),
        )
        relay_u = lax.dynamic_index_in_dim(
            row_u.reshape(tiles_col, col_ratio, rank_width, tile_order),
            pick_slot,
            1,
            keepdims=False,
        )
        relay_v = lax.dynamic_index_in_dim(
            row_raw.reshape(tiles_col, col_ratio, rank_width, tile_order),
            pick_slot,
            1,
            keepdims=False,
        )
        own_chol = lax.cond(row_index == diag_owner, factor_tile, zero_tile, whole_tile)
        whole_tile = None
        relay_here = row_index == col_index % row_count
        relay = jnp.concatenate([relay_u, relay_v], axis=0).astype(jnp.float32)
        relay = jnp.where(relay_here, relay, jnp.zeros_like(relay))
        own_chol = jnp.where(row_index == diag_owner, own_chol, jnp.zeros_like(own_chol))
        merged = lax.psum(
            jnp.concatenate([own_chol, relay.reshape(-1, tile_order)], axis=0), "row"
        )
        chol_k = merged[:tile_order]
        relay = merged[tile_order:].reshape(relay.shape).astype(jnp.bfloat16)
        col_u = relay[:tiles_col]
        col_raw = relay[tiles_col:]
        solved = solve_packed(chol_k, jnp.concatenate([row_raw, col_raw], axis=0))
        row_v = solved[:tiles_row]
        col_v = solved[tiles_row:]
        row_live = (row_tile > panel_index)[:, None, None]
        col_live = (col_tile > panel_index)[:, None, None]
        row_u = jnp.where(row_live, row_u, zero_bf)
        row_v = jnp.where(row_live, row_v, zero_bf)
        col_u = jnp.where(col_live, col_u, zero_bf)
        col_v = jnp.where(col_live, col_v, zero_bf)
        self_c = jnp.einsum(
            "arx,asx->ars", row_v, row_v, preferred_element_type=jnp.float32
        ).astype(jnp.bfloat16)
        spread = jnp.einsum(
            "ars,asx->arx", self_c, row_u, preferred_element_type=jnp.float32
        ).astype(jnp.bfloat16)
        part_u = lax.dynamic_slice_in_dim(row_u, first_row, diag_rows, 2)
        lowered = diagonal - jnp.einsum(
            "arx,ary->axy", part_u, spread, preferred_element_type=jnp.float32
        )
        chol_rows = lax.dynamic_slice_in_dim(chol_k, first_row, diag_rows, 0)
        chol_rows = jnp.where(chol_cols <= chol_rows_at, chol_rows, 0.0)
        diag_tile = row_tile[:, None, None]
        diagonal = jnp.where(
            diag_tile > panel_index,
            lowered,
            jnp.where(diag_tile == panel_index, chol_rows[None], diagonal),
        )
        if panel_index + 1 < PANELS:
            next_slot = (panel_index + 1) // row_count
            whole_tile = lax.all_gather(diagonal[next_slot], "col", axis=0, tiled=True)
        coupling = jnp.einsum("arx,bsx->abrs", row_v, col_v, preferred_element_type=jnp.float32)
        col_sketch = jnp.einsum("rx,bsx->brs", sketch, col_u, preferred_element_type=jnp.float32)
        sketch_v = jnp.einsum(
            "rx,absx->abrs", sketch, factor_v, preferred_element_type=jnp.float32
        ).astype(jnp.bfloat16)
        sketch_c = jnp.einsum("brs,abts->abrt", col_sketch, coupling, precision=highest).astype(
            jnp.bfloat16
        )
        range_y = jnp.einsum(
            "abrs,absx->abrx", sketch_v, factor_u, preferred_element_type=jnp.float32
        )
        range_y = range_y - jnp.einsum(
            "abrs,asx->abrx", sketch_c, row_u, preferred_element_type=jnp.float32
        )
        keep_rows = rank_slots[None, None, :] < rank_levels[panel_index + 1][:, :, None]
        range_y = jnp.where(keep_rows[..., None], range_y, 0.0).astype(jnp.bfloat16)
        gram_matrix = jnp.einsum(
            "abrx,absx->abrs", range_y, range_y, preferred_element_type=jnp.float32
        )
        gram_matrix = gram_matrix + (1.0 - keep_rows.astype(jnp.float32))[..., None] * identity
        proj_u = jnp.einsum(
            "abrx,absx->abrs", range_y, factor_u, preferred_element_type=jnp.float32
        )
        proj_own = jnp.einsum("abrx,asx->abrs", range_y, row_u, preferred_element_type=jnp.float32)
        proj_c = jnp.einsum("abrs,abst->abrt", proj_own, coupling, precision=highest)
        gram_inv = factor_inverse(gram_matrix)
        both = jnp.concatenate([proj_u, proj_c], axis=-1)
        middle = jnp.einsum("abrs,abst->abrt", gram_inv, both, precision=highest)
        cores = jnp.einsum("absr,abst->abrt", gram_inv, middle, precision=highest)
        first_core = cores[..., :rank_width].astype(jnp.bfloat16)
        second_core = cores[..., rank_width:].astype(jnp.bfloat16)
        fresh_v = jnp.einsum(
            "abrs,absx->abrx", first_core, factor_v, preferred_element_type=jnp.float32
        )
        fresh_v = (
            fresh_v
            - jnp.einsum("abrs,bsx->abrx", second_core, col_u, preferred_element_type=jnp.float32)
        ).astype(jnp.bfloat16)
        if whole_tile is not None:
            whole_tile, fresh_v = lax.optimization_barrier((whole_tile, fresh_v))
        update_mask = ((row_tile[:, None] > col_tile[None, :]) & (col_tile[None, :] > panel_index))[
            ..., None, None
        ]
        at_panel = ((col_tile[None, :] == panel_index) & (row_tile[:, None] > panel_index))[
            ..., None, None
        ]
        factor_u = jnp.where(update_mask, range_y, jnp.where(at_panel, row_u[:, None], factor_u))
        factor_v = jnp.where(update_mask, fresh_v, jnp.where(at_panel, row_v[:, None], factor_v))
    return (factor_u, factor_v, diagonal)


def solution(mesh):
    in_specs = (
        P("row", "col", None, None),
        P("row", "col", None, None),
        P("row", "col", None),
        P(),
        P(None, "row", "col"),
    )
    out_specs = (P("row", "col", None, None), P("row", "col", None, None), P("row", "col", None))
    return jax.shard_map(
        on_device, mesh=mesh, in_specs=in_specs, out_specs=out_specs, check_vma=False
    )
```

```python
import jax
import jax.numpy as jnp
from jax import lax
from jax.sharding import PartitionSpec as P

PANELS = 2


highest = lax.Precision.HIGHEST
fine = lax.Precision.HIGH


def broadcast(shard, axis, root):
    mine = lax.axis_index(axis) == root
    return lax.psum(jnp.where(mine, shard, jnp.zeros_like(shard)), axis)


def chol_apply(factor, rhs):
    middle = jax.scipy.linalg.solve_triangular(factor, rhs, lower=True)
    return jax.scipy.linalg.solve_triangular(factor, middle, lower=True, trans=1)


def solve_panel(chol_k, raw_factors):
    tile_count, rank_width, tile_order = raw_factors.shape
    flattened = raw_factors.reshape(tile_count * rank_width, tile_order).astype(jnp.float32).T
    solved = jax.scipy.linalg.solve_triangular(chol_k, flattened, lower=True)
    return solved.T.reshape(tile_count, rank_width, tile_order).astype(jnp.bfloat16)


BLOCK = 128


def factor_tile(tile_mat):
    order = tile_mat.shape[0]
    width = min(BLOCK, order)
    count = order // width
    work = (tile_mat + tile_mat.T) * 0.5
    eye = jnp.eye(width, dtype=jnp.float32)
    strips = []
    for step in range(count):
        head = jnp.tril(lax.linalg.cholesky(work[:width, :width], symmetrize_input=False))
        head_inv = lax.linalg.triangular_solve(head, eye, left_side=True, lower=True)
        parts = [jnp.zeros((step * width, width), jnp.float32), head + jnp.triu(head_inv.T, 1)]
        if step < count - 1:
            below = jnp.dot(work[width:, :width], head_inv.T, precision=fine)
            work = work[width:, width:] - jnp.dot(below, below.T, precision=fine)
            parts.append(below)
        strips.append(jnp.concatenate(parts, axis=0))
    return jnp.concatenate(strips, axis=1)


def factor_inverse(gram):
    order = gram.shape[-1]
    width = min(BLOCK, order)
    gram = (gram + jnp.swapaxes(gram, -1, -2)) * 0.5
    eye = jnp.broadcast_to(jnp.eye(width, dtype=jnp.float32), gram.shape[:-2] + (width, width))
    head = jnp.tril(lax.linalg.cholesky(gram[..., :width, :width], symmetrize_input=False))
    head_inv = lax.linalg.triangular_solve(head, eye, left_side=True, lower=True)
    if width == order:
        return head_inv
    rest = order - width
    below = jnp.einsum("...ij,...kj->...ik", gram[..., width:, :width], head_inv, precision=highest)
    tail = gram[..., width:, width:] - jnp.einsum("...ij,...kj->...ik", below, below, precision=highest)
    tail = jnp.tril(lax.linalg.cholesky(tail, symmetrize_input=False))
    eye_rest = jnp.broadcast_to(jnp.eye(rest, dtype=jnp.float32), gram.shape[:-2] + (rest, rest))
    tail_inv = lax.linalg.triangular_solve(tail, eye_rest, left_side=True, lower=True)
    cross = jnp.einsum("...ij,...jk->...ik", below, head_inv, precision=highest)
    cross = -jnp.einsum("...ij,...jk->...ik", tail_inv, cross, precision=highest)
    top = jnp.concatenate([head_inv, jnp.zeros(gram.shape[:-2] + (width, rest), jnp.float32)], -1)
    return jnp.concatenate([top, jnp.concatenate([cross, tail_inv], -1)], -2)


def skip_inverse(gram):
    return jnp.broadcast_to(jnp.eye(gram.shape[-1], dtype=jnp.float32), gram.shape)


def solve_packed(packed, raw_factors):
    order = packed.shape[0]
    width = min(BLOCK, order)
    count = order // width
    lead = raw_factors.shape[:-1]
    rows = raw_factors.reshape(-1, order).astype(jnp.float32)
    done = []
    for step in range(count):
        lo, hi = step * width, (step + 1) * width
        block = packed[lo:hi, lo:hi]
        inverse = jnp.tril(block.T, -1) + jnp.diag(1.0 / jnp.diagonal(block))
        rhs = rows[:, lo:hi]
        if step:
            prior = jnp.concatenate(done, axis=1)
            rhs = rhs - jnp.dot(prior, packed[lo:hi, :lo].T, precision=fine)
        done.append(jnp.dot(rhs, inverse.T, precision=fine))
    return jnp.concatenate(done, axis=1).reshape(lead + (order,)).astype(jnp.bfloat16)


def zero_tile(tile_mat):
    return jnp.zeros_like(tile_mat)


def zero_factors(chol_k, raw_factors):
    return jnp.zeros_like(raw_factors)


def on_device(u_factors, v_factors, diag_tiles, sketch, rank_levels):
    row_count = lax.axis_size("row")
    col_count = lax.axis_size("col")
    row_index = lax.axis_index("row")
    col_index = lax.axis_index("col")
    tiles_row, tiles_col, rank_width, tile_order = u_factors.shape
    diag_rows = diag_tiles.shape[1]
    col_ratio = col_count // row_count
    row_tile = jnp.arange(tiles_row, dtype=jnp.int32) * row_count + row_index
    col_tile = jnp.arange(tiles_col, dtype=jnp.int32) * col_count + col_index
    rank_slots = jnp.arange(rank_width, dtype=jnp.int32)
    identity = jnp.eye(rank_width, dtype=jnp.float32)
    zero_bf = jnp.zeros((), jnp.bfloat16)
    below_diag = row_tile[:, None] > col_tile[None, :]
    live_rows = (rank_slots[None, None, :] < rank_levels[0][:, :, None]) & below_diag[:, :, None]
    factor_u = jnp.where(live_rows[..., None], u_factors, zero_bf)
    factor_v = jnp.where(live_rows[..., None], v_factors, zero_bf)
    diagonal = diag_tiles
    first_row = col_index * diag_rows
    pick_slot = col_index // row_count
    chol_cols = jnp.arange(tile_order, dtype=jnp.int32)[None, :]
    chol_rows_at = first_row + jnp.arange(diag_rows, dtype=jnp.int32)[:, None]
    whole_tile = None
    for panel_index in range(PANELS):
        diag_slot = panel_index // row_count
        diag_owner = panel_index % row_count
        col_slot = panel_index // col_count
        col_owner = panel_index % col_count
        raw_u = factor_u[:, col_slot]
        raw_v = factor_v[:, col_slot]
        if whole_tile is None:
            whole_tile = lax.all_gather(diagonal[diag_slot], "col", axis=0, tiled=True)
            whole_tile, raw_u, raw_v = lax.optimization_barrier((whole_tile, raw_u, raw_v))
        row_u, row_raw = (
            broadcast(raw_u, "col", col_owner),
            broadcast(raw_v, "col", col_owner),
        )
        relay_u = lax.dynamic_index_in_dim(
            row_u.reshape(tiles_col, col_ratio, rank_width, tile_order),
            pick_slot,
            1,
            keepdims=False,
        )
        relay_v = lax.dynamic_index_in_dim(
            row_raw.reshape(tiles_col, col_ratio, rank_width, tile_order),
            pick_slot,
            1,
            keepdims=False,
        )
        own_chol = lax.cond(row_index == diag_owner, factor_tile, zero_tile, whole_tile)
        whole_tile = None
        relay_here = row_index == col_index % row_count
        relay = jnp.concatenate([relay_u, relay_v], axis=0).astype(jnp.float32)
        relay = jnp.where(relay_here, relay, jnp.zeros_like(relay))
        own_chol = jnp.where(row_index == diag_owner, own_chol, jnp.zeros_like(own_chol))
        merged = lax.psum(
            jnp.concatenate([own_chol, relay.reshape(-1, tile_order)], axis=0), "row"
        )
        chol_k = merged[:tile_order]
        relay = merged[tile_order:].reshape(relay.shape).astype(jnp.bfloat16)
        col_u = relay[:tiles_col]
        col_raw = relay[tiles_col:]
        solved = solve_packed(chol_k, jnp.concatenate([row_raw, col_raw], axis=0))
        row_v = solved[:tiles_row]
        col_v = solved[tiles_row:]
        row_live = (row_tile > panel_index)[:, None, None]
        col_live = (col_tile > panel_index)[:, None, None]
        row_u = jnp.where(row_live, row_u, zero_bf)
        row_v = jnp.where(row_live, row_v, zero_bf)
        col_u = jnp.where(col_live, col_u, zero_bf)
        col_v = jnp.where(col_live, col_v, zero_bf)
        self_c = jnp.einsum(
            "arx,asx->ars", row_v, row_v, preferred_element_type=jnp.float32
        ).astype(jnp.bfloat16)
        spread = jnp.einsum(
            "ars,asx->arx", self_c, row_u, preferred_element_type=jnp.float32
        ).astype(jnp.bfloat16)
        part_u = lax.dynamic_slice_in_dim(row_u, first_row, diag_rows, 2)
        lowered = diagonal - jnp.einsum(
            "arx,ary->axy", part_u, spread, preferred_element_type=jnp.float32
        )
        chol_rows = lax.dynamic_slice_in_dim(chol_k, first_row, diag_rows, 0)
        chol_rows = jnp.where(chol_cols <= chol_rows_at, chol_rows, 0.0)
        diag_tile = row_tile[:, None, None]
        diagonal = jnp.where(
            diag_tile > panel_index,
            lowered,
            jnp.where(diag_tile == panel_index, chol_rows[None], diagonal),
        )
        if panel_index + 1 < PANELS:
            next_slot = (panel_index + 1) // row_count
            whole_tile = lax.all_gather(diagonal[next_slot], "col", axis=0, tiled=True)
        coupling = jnp.einsum("arx,bsx->abrs", row_v, col_v, preferred_element_type=jnp.float32)
        col_sketch = jnp.einsum("rx,bsx->brs", sketch, col_u, preferred_element_type=jnp.float32)
        sketch_v = jnp.einsum(
            "rx,absx->abrs", sketch, factor_v, preferred_element_type=jnp.float32
        ).astype(jnp.bfloat16)
        sketch_c = jnp.einsum("brs,abts->abrt", col_sketch, coupling, precision=highest).astype(
            jnp.bfloat16
        )
        range_y = jnp.einsum(
            "abrs,absx->abrx", sketch_v, factor_u, preferred_element_type=jnp.float32
        )
        range_y = range_y - jnp.einsum(
            "abrs,asx->abrx", sketch_c, row_u, preferred_element_type=jnp.float32
        )
        keep_rows = rank_slots[None, None, :] < rank_levels[panel_index + 1][:, :, None]
        range_y = jnp.where(keep_rows[..., None], range_y, 0.0).astype(jnp.bfloat16)
        gram_matrix = jnp.einsum(
            "abrx,absx->abrs", range_y, range_y, preferred_element_type=jnp.float32
        )
        gram_matrix = gram_matrix + (1.0 - keep_rows.astype(jnp.float32))[..., None] * identity
        proj_u = jnp.einsum(
            "abrx,absx->abrs", range_y, factor_u, preferred_element_type=jnp.float32
        )
        proj_own = jnp.einsum("abrx,asx->abrs", range_y, row_u, preferred_element_type=jnp.float32)
        proj_c = jnp.einsum("abrs,abst->abrt", proj_own, coupling, precision=highest)
        update_live = (row_tile[:, None] > col_tile[None, :]) & (col_tile[None, :] > panel_index)
        inv_parts = []
        for slot in range(tiles_row):
            for cslot in range(tiles_col):
                inv_parts.append(
                    lax.cond(
                        update_live[slot, cslot],
                        factor_inverse,
                        skip_inverse,
                        gram_matrix[slot, cslot],
                    )
                )
        gram_inv = jnp.stack(inv_parts).reshape(gram_matrix.shape)
        both = jnp.concatenate([proj_u, proj_c], axis=-1)
        middle = jnp.einsum("abrs,abst->abrt", gram_inv, both, precision=highest)
        cores = jnp.einsum("absr,abst->abrt", gram_inv, middle, precision=highest)
        first_core = cores[..., :rank_width].astype(jnp.bfloat16)
        second_core = cores[..., rank_width:].astype(jnp.bfloat16)
        fresh_v = jnp.einsum(
            "abrs,absx->abrx", first_core, factor_v, preferred_element_type=jnp.float32
        )
        fresh_v = (
            fresh_v
            - jnp.einsum("abrs,bsx->abrx", second_core, col_u, preferred_element_type=jnp.float32)
        ).astype(jnp.bfloat16)
        if whole_tile is not None:
            whole_tile, fresh_v = lax.optimization_barrier((whole_tile, fresh_v))
        update_mask = ((row_tile[:, None] > col_tile[None, :]) & (col_tile[None, :] > panel_index))[
            ..., None, None
        ]
        at_panel = ((col_tile[None, :] == panel_index) & (row_tile[:, None] > panel_index))[
            ..., None, None
        ]
        factor_u = jnp.where(update_mask, range_y, jnp.where(at_panel, row_u[:, None], factor_u))
        factor_v = jnp.where(update_mask, fresh_v, jnp.where(at_panel, row_v[:, None], factor_v))
    return (factor_u, factor_v, diagonal)


def solution(mesh):
    in_specs = (
        P("row", "col", None, None),
        P("row", "col", None, None),
        P("row", "col", None),
        P(),
        P(None, "row", "col"),
    )
    out_specs = (P("row", "col", None, None), P("row", "col", None, None), P("row", "col", None))
    return jax.shard_map(
        on_device, mesh=mesh, in_specs=in_specs, out_specs=out_specs, check_vma=False
    )
```

```python
import jax
import jax.numpy as jnp
from jax import lax
from jax.sharding import PartitionSpec as P

PANELS = 2


highest = lax.Precision.HIGHEST
fine = lax.Precision.HIGH


def broadcast(shard, axis, root):
    mine = lax.axis_index(axis) == root
    return lax.psum(jnp.where(mine, shard, jnp.zeros_like(shard)), axis)


def chol_apply(factor, rhs):
    middle = jax.scipy.linalg.solve_triangular(factor, rhs, lower=True)
    return jax.scipy.linalg.solve_triangular(factor, middle, lower=True, trans=1)


def solve_panel(chol_k, raw_factors):
    tile_count, rank_width, tile_order = raw_factors.shape
    flattened = raw_factors.reshape(tile_count * rank_width, tile_order).astype(jnp.float32).T
    solved = jax.scipy.linalg.solve_triangular(chol_k, flattened, lower=True)
    return solved.T.reshape(tile_count, rank_width, tile_order).astype(jnp.bfloat16)


BLOCK = 128


def factor_tile(tile_mat):
    order = tile_mat.shape[0]
    width = min(BLOCK, order)
    count = order // width
    work = (tile_mat + tile_mat.T) * 0.5
    eye = jnp.eye(width, dtype=jnp.float32)
    strips = []
    for step in range(count):
        head = jnp.tril(lax.linalg.cholesky(work[:width, :width], symmetrize_input=False))
        head_inv = lax.linalg.triangular_solve(head, eye, left_side=True, lower=True)
        parts = [jnp.zeros((step * width, width), jnp.float32), head + jnp.triu(head_inv.T, 1)]
        if step < count - 1:
            below = jnp.dot(work[width:, :width], head_inv.T, precision=fine)
            work = work[width:, width:] - jnp.dot(below, below.T, precision=fine)
            parts.append(below)
        strips.append(jnp.concatenate(parts, axis=0))
    return jnp.concatenate(strips, axis=1)


def factor_inverse(gram):
    order = gram.shape[-1]
    width = min(BLOCK, order)
    gram = (gram + jnp.swapaxes(gram, -1, -2)) * 0.5
    eye = jnp.broadcast_to(jnp.eye(width, dtype=jnp.float32), gram.shape[:-2] + (width, width))
    head = jnp.tril(lax.linalg.cholesky(gram[..., :width, :width], symmetrize_input=False))
    head_inv = lax.linalg.triangular_solve(head, eye, left_side=True, lower=True)
    if width == order:
        return head_inv
    rest = order - width
    below = jnp.einsum("...ij,...kj->...ik", gram[..., width:, :width], head_inv, precision=highest)
    tail = gram[..., width:, width:] - jnp.einsum("...ij,...kj->...ik", below, below, precision=highest)
    tail = jnp.tril(lax.linalg.cholesky(tail, symmetrize_input=False))
    eye_rest = jnp.broadcast_to(jnp.eye(rest, dtype=jnp.float32), gram.shape[:-2] + (rest, rest))
    tail_inv = lax.linalg.triangular_solve(tail, eye_rest, left_side=True, lower=True)
    cross = jnp.einsum("...ij,...jk->...ik", below, head_inv, precision=highest)
    cross = -jnp.einsum("...ij,...jk->...ik", tail_inv, cross, precision=highest)
    top = jnp.concatenate([head_inv, jnp.zeros(gram.shape[:-2] + (width, rest), jnp.float32)], -1)
    return jnp.concatenate([top, jnp.concatenate([cross, tail_inv], -1)], -2)


def solve_packed(packed, raw_factors):
    order = packed.shape[0]
    width = min(BLOCK, order)
    count = order // width
    lead = raw_factors.shape[:-1]
    rest = raw_factors.reshape(-1, order).astype(jnp.float32)
    done = []
    for step in range(count):
        lo, hi = step * width, (step + 1) * width
        block = packed[lo:hi, lo:hi]
        inverse = jnp.tril(block.T, -1) + jnp.diag(1.0 / jnp.diagonal(block))
        part = jnp.dot(rest[:, :width], inverse.T, precision=fine)
        done.append(part)
        if step < count - 1:
            rest = rest[:, width:] - jnp.dot(part, packed[hi:, lo:hi].T, precision=fine)
    return jnp.concatenate(done, axis=1).reshape(lead + (order,)).astype(jnp.bfloat16)


def zero_tile(tile_mat):
    return jnp.zeros_like(tile_mat)


def zero_factors(chol_k, raw_factors):
    return jnp.zeros_like(raw_factors)


def on_device(u_factors, v_factors, diag_tiles, sketch, rank_levels):
    row_count = lax.axis_size("row")
    col_count = lax.axis_size("col")
    row_index = lax.axis_index("row")
    col_index = lax.axis_index("col")
    tiles_row, tiles_col, rank_width, tile_order = u_factors.shape
    diag_rows = diag_tiles.shape[1]
    col_ratio = col_count // row_count
    row_tile = jnp.arange(tiles_row, dtype=jnp.int32) * row_count + row_index
    col_tile = jnp.arange(tiles_col, dtype=jnp.int32) * col_count + col_index
    rank_slots = jnp.arange(rank_width, dtype=jnp.int32)
    identity = jnp.eye(rank_width, dtype=jnp.float32)
    zero_bf = jnp.zeros((), jnp.bfloat16)
    below_diag = row_tile[:, None] > col_tile[None, :]
    live_rows = (rank_slots[None, None, :] < rank_levels[0][:, :, None]) & below_diag[:, :, None]
    factor_u = jnp.where(live_rows[..., None], u_factors, zero_bf)
    factor_v = jnp.where(live_rows[..., None], v_factors, zero_bf)
    diagonal = diag_tiles
    first_row = col_index * diag_rows
    pick_slot = col_index // row_count
    chol_cols = jnp.arange(tile_order, dtype=jnp.int32)[None, :]
    chol_rows_at = first_row + jnp.arange(diag_rows, dtype=jnp.int32)[:, None]
    whole_tile = None
    for panel_index in range(PANELS):
        diag_slot = panel_index // row_count
        diag_owner = panel_index % row_count
        col_slot = panel_index // col_count
        col_owner = panel_index % col_count
        raw_u = factor_u[:, col_slot]
        raw_v = factor_v[:, col_slot]
        if whole_tile is None:
            whole_tile = lax.all_gather(diagonal[diag_slot], "col", axis=0, tiled=True)
            whole_tile, raw_u, raw_v = lax.optimization_barrier((whole_tile, raw_u, raw_v))
        row_u, row_raw = (
            broadcast(raw_u, "col", col_owner),
            broadcast(raw_v, "col", col_owner),
        )
        relay_u = lax.dynamic_index_in_dim(
            row_u.reshape(tiles_col, col_ratio, rank_width, tile_order),
            pick_slot,
            1,
            keepdims=False,
        )
        relay_v = lax.dynamic_index_in_dim(
            row_raw.reshape(tiles_col, col_ratio, rank_width, tile_order),
            pick_slot,
            1,
            keepdims=False,
        )
        own_chol = lax.cond(row_index == diag_owner, factor_tile, zero_tile, whole_tile)
        whole_tile = None
        relay_here = row_index == col_index % row_count
        relay = jnp.concatenate([relay_u, relay_v], axis=0).astype(jnp.float32)
        relay = jnp.where(relay_here, relay, jnp.zeros_like(relay))
        own_chol = jnp.where(row_index == diag_owner, own_chol, jnp.zeros_like(own_chol))
        merged = lax.psum(
            jnp.concatenate([own_chol, relay.reshape(-1, tile_order)], axis=0), "row"
        )
        chol_k = merged[:tile_order]
        relay = merged[tile_order:].reshape(relay.shape).astype(jnp.bfloat16)
        col_u = relay[:tiles_col]
        col_raw = relay[tiles_col:]
        solved = solve_packed(chol_k, jnp.concatenate([row_raw, col_raw], axis=0))
        row_v = solved[:tiles_row]
        col_v = solved[tiles_row:]
        row_live = (row_tile > panel_index)[:, None, None]
        col_live = (col_tile > panel_index)[:, None, None]
        row_u = jnp.where(row_live, row_u, zero_bf)
        row_v = jnp.where(row_live, row_v, zero_bf)
        col_u = jnp.where(col_live, col_u, zero_bf)
        col_v = jnp.where(col_live, col_v, zero_bf)
        self_c = jnp.einsum(
            "arx,asx->ars", row_v, row_v, preferred_element_type=jnp.float32
        ).astype(jnp.bfloat16)
        spread = jnp.einsum(
            "ars,asx->arx", self_c, row_u, preferred_element_type=jnp.float32
        ).astype(jnp.bfloat16)
        part_u = lax.dynamic_slice_in_dim(row_u, first_row, diag_rows, 2)
        lowered = diagonal - jnp.einsum(
            "arx,ary->axy", part_u, spread, preferred_element_type=jnp.float32
        )
        chol_rows = lax.dynamic_slice_in_dim(chol_k, first_row, diag_rows, 0)
        chol_rows = jnp.where(chol_cols <= chol_rows_at, chol_rows, 0.0)
        diag_tile = row_tile[:, None, None]
        diagonal = jnp.where(
            diag_tile > panel_index,
            lowered,
            jnp.where(diag_tile == panel_index, chol_rows[None], diagonal),
        )
        if panel_index + 1 < PANELS:
            next_slot = (panel_index + 1) // row_count
            whole_tile = lax.all_gather(diagonal[next_slot], "col", axis=0, tiled=True)
        coupling = jnp.einsum("arx,bsx->abrs", row_v, col_v, preferred_element_type=jnp.float32)
        col_sketch = jnp.einsum("rx,bsx->brs", sketch, col_u, preferred_element_type=jnp.float32)
        sketch_v = jnp.einsum(
            "rx,absx->abrs", sketch, factor_v, preferred_element_type=jnp.float32
        ).astype(jnp.bfloat16)
        sketch_c = jnp.einsum("brs,abts->abrt", col_sketch, coupling, precision=highest).astype(
            jnp.bfloat16
        )
        range_y = jnp.einsum(
            "abrs,absx->abrx", sketch_v, factor_u, preferred_element_type=jnp.float32
        )
        range_y = range_y - jnp.einsum(
            "abrs,asx->abrx", sketch_c, row_u, preferred_element_type=jnp.float32
        )
        keep_rows = rank_slots[None, None, :] < rank_levels[panel_index + 1][:, :, None]
        range_y = jnp.where(keep_rows[..., None], range_y, 0.0).astype(jnp.bfloat16)
        gram_matrix = jnp.einsum(
            "abrx,absx->abrs", range_y, range_y, preferred_element_type=jnp.float32
        )
        gram_matrix = gram_matrix + (1.0 - keep_rows.astype(jnp.float32))[..., None] * identity
        proj_u = jnp.einsum(
            "abrx,absx->abrs", range_y, factor_u, preferred_element_type=jnp.float32
        )
        proj_own = jnp.einsum("abrx,asx->abrs", range_y, row_u, preferred_element_type=jnp.float32)
        proj_c = jnp.einsum("abrs,abst->abrt", proj_own, coupling, precision=highest)
        gram_inv = factor_inverse(gram_matrix)
        both = jnp.concatenate([proj_u, proj_c], axis=-1)
        middle = jnp.einsum("abrs,abst->abrt", gram_inv, both, precision=highest)
        cores = jnp.einsum("absr,abst->abrt", gram_inv, middle, precision=highest)
        first_core = cores[..., :rank_width].astype(jnp.bfloat16)
        second_core = cores[..., rank_width:].astype(jnp.bfloat16)
        fresh_v = jnp.einsum(
            "abrs,absx->abrx", first_core, factor_v, preferred_element_type=jnp.float32
        )
        fresh_v = (
            fresh_v
            - jnp.einsum("abrs,bsx->abrx", second_core, col_u, preferred_element_type=jnp.float32)
        ).astype(jnp.bfloat16)
        if whole_tile is not None:
            whole_tile, fresh_v = lax.optimization_barrier((whole_tile, fresh_v))
        update_mask = ((row_tile[:, None] > col_tile[None, :]) & (col_tile[None, :] > panel_index))[
            ..., None, None
        ]
        at_panel = ((col_tile[None, :] == panel_index) & (row_tile[:, None] > panel_index))[
            ..., None, None
        ]
        factor_u = jnp.where(update_mask, range_y, jnp.where(at_panel, row_u[:, None], factor_u))
        factor_v = jnp.where(update_mask, fresh_v, jnp.where(at_panel, row_v[:, None], factor_v))
    return (factor_u, factor_v, diagonal)


def solution(mesh):
    in_specs = (
        P("row", "col", None, None),
        P("row", "col", None, None),
        P("row", "col", None),
        P(),
        P(None, "row", "col"),
    )
    out_specs = (P("row", "col", None, None), P("row", "col", None, None), P("row", "col", None))
    return jax.shard_map(
        on_device, mesh=mesh, in_specs=in_specs, out_specs=out_specs, check_vma=False
    )
```

```python
import jax
import jax.numpy as jnp
from jax import lax
from jax.sharding import PartitionSpec as P

PANELS = 2


highest = lax.Precision.HIGHEST
fine = lax.Precision.HIGH


def broadcast(shard, axis, root):
    mine = lax.axis_index(axis) == root
    return lax.psum(jnp.where(mine, shard, jnp.zeros_like(shard)), axis)


def chol_apply(factor, rhs):
    middle = jax.scipy.linalg.solve_triangular(factor, rhs, lower=True)
    return jax.scipy.linalg.solve_triangular(factor, middle, lower=True, trans=1)


def solve_panel(chol_k, raw_factors):
    tile_count, rank_width, tile_order = raw_factors.shape
    flattened = raw_factors.reshape(tile_count * rank_width, tile_order).astype(jnp.float32).T
    solved = jax.scipy.linalg.solve_triangular(chol_k, flattened, lower=True)
    return solved.T.reshape(tile_count, rank_width, tile_order).astype(jnp.bfloat16)


BLOCK = 128


def factor_tile(tile_mat):
    order = tile_mat.shape[0]
    width = min(BLOCK, order)
    count = order // width
    sym = (tile_mat + tile_mat.T) * 0.5
    eye = jnp.eye(width, dtype=jnp.float32)
    packed = jnp.zeros((order, order), jnp.float32)
    for step in range(count):
        lo, hi = step * width, (step + 1) * width
        column = sym[lo:, lo:hi]
        if step:
            column = column - jnp.dot(packed[lo:, :lo], packed[lo:hi, :lo].T, precision=fine)
        head = jnp.tril(lax.linalg.cholesky(column[:width], symmetrize_input=False))
        head_inv = lax.linalg.triangular_solve(head, eye, left_side=True, lower=True)
        block = head + jnp.triu(head_inv.T, 1)
        if step < count - 1:
            below = jnp.dot(column[width:], head_inv.T, precision=fine)
            block = jnp.concatenate([block, below], axis=0)
        packed = lax.dynamic_update_slice(packed, block, (lo, lo))
    return packed


def factor_inverse(gram):
    order = gram.shape[-1]
    width = min(BLOCK, order)
    gram = (gram + jnp.swapaxes(gram, -1, -2)) * 0.5
    eye = jnp.broadcast_to(jnp.eye(width, dtype=jnp.float32), gram.shape[:-2] + (width, width))
    head = jnp.tril(lax.linalg.cholesky(gram[..., :width, :width], symmetrize_input=False))
    head_inv = lax.linalg.triangular_solve(head, eye, left_side=True, lower=True)
    if width == order:
        return head_inv
    rest = order - width
    below = jnp.einsum("...ij,...kj->...ik", gram[..., width:, :width], head_inv, precision=highest)
    tail = gram[..., width:, width:] - jnp.einsum("...ij,...kj->...ik", below, below, precision=highest)
    tail = jnp.tril(lax.linalg.cholesky(tail, symmetrize_input=False))
    eye_rest = jnp.broadcast_to(jnp.eye(rest, dtype=jnp.float32), gram.shape[:-2] + (rest, rest))
    tail_inv = lax.linalg.triangular_solve(tail, eye_rest, left_side=True, lower=True)
    cross = jnp.einsum("...ij,...jk->...ik", below, head_inv, precision=highest)
    cross = -jnp.einsum("...ij,...jk->...ik", tail_inv, cross, precision=highest)
    top = jnp.concatenate([head_inv, jnp.zeros(gram.shape[:-2] + (width, rest), jnp.float32)], -1)
    return jnp.concatenate([top, jnp.concatenate([cross, tail_inv], -1)], -2)


def solve_packed(packed, raw_factors):
    order = packed.shape[0]
    width = min(BLOCK, order)
    count = order // width
    lead = raw_factors.shape[:-1]
    rest = raw_factors.reshape(-1, order).astype(jnp.float32)
    done = []
    for step in range(count):
        lo, hi = step * width, (step + 1) * width
        block = packed[lo:hi, lo:hi]
        inverse = jnp.tril(block.T, -1) + jnp.diag(1.0 / jnp.diagonal(block))
        part = jnp.dot(rest[:, :width], inverse.T, precision=fine)
        done.append(part)
        if step < count - 1:
            rest = rest[:, width:] - jnp.dot(part, packed[hi:, lo:hi].T, precision=fine)
    return jnp.concatenate(done, axis=1).reshape(lead + (order,)).astype(jnp.bfloat16)


def zero_tile(tile_mat):
    return jnp.zeros_like(tile_mat)


def zero_factors(chol_k, raw_factors):
    return jnp.zeros_like(raw_factors)


def on_device(u_factors, v_factors, diag_tiles, sketch, rank_levels):
    row_count = lax.axis_size("row")
    col_count = lax.axis_size("col")
    row_index = lax.axis_index("row")
    col_index = lax.axis_index("col")
    tiles_row, tiles_col, rank_width, tile_order = u_factors.shape
    diag_rows = diag_tiles.shape[1]
    col_ratio = col_count // row_count
    row_tile = jnp.arange(tiles_row, dtype=jnp.int32) * row_count + row_index
    col_tile = jnp.arange(tiles_col, dtype=jnp.int32) * col_count + col_index
    rank_slots = jnp.arange(rank_width, dtype=jnp.int32)
    identity = jnp.eye(rank_width, dtype=jnp.float32)
    zero_bf = jnp.zeros((), jnp.bfloat16)
    below_diag = row_tile[:, None] > col_tile[None, :]
    live_rows = (rank_slots[None, None, :] < rank_levels[0][:, :, None]) & below_diag[:, :, None]
    factor_u = jnp.where(live_rows[..., None], u_factors, zero_bf)
    factor_v = jnp.where(live_rows[..., None], v_factors, zero_bf)
    diagonal = diag_tiles
    first_row = col_index * diag_rows
    pick_slot = col_index // row_count
    chol_cols = jnp.arange(tile_order, dtype=jnp.int32)[None, :]
    chol_rows_at = first_row + jnp.arange(diag_rows, dtype=jnp.int32)[:, None]
    whole_tile = None
    for panel_index in range(PANELS):
        diag_slot = panel_index // row_count
        diag_owner = panel_index % row_count
        col_slot = panel_index // col_count
        col_owner = panel_index % col_count
        raw_u = factor_u[:, col_slot]
        raw_v = factor_v[:, col_slot]
        if whole_tile is None:
            whole_tile = lax.all_gather(diagonal[diag_slot], "col", axis=0, tiled=True)
            whole_tile, raw_u, raw_v = lax.optimization_barrier((whole_tile, raw_u, raw_v))
        row_u, row_raw = (
            broadcast(raw_u, "col", col_owner),
            broadcast(raw_v, "col", col_owner),
        )
        relay_u = lax.dynamic_index_in_dim(
            row_u.reshape(tiles_col, col_ratio, rank_width, tile_order),
            pick_slot,
            1,
            keepdims=False,
        )
        relay_v = lax.dynamic_index_in_dim(
            row_raw.reshape(tiles_col, col_ratio, rank_width, tile_order),
            pick_slot,
            1,
            keepdims=False,
        )
        own_chol = lax.cond(row_index == diag_owner, factor_tile, zero_tile, whole_tile)
        whole_tile = None
        relay_here = row_index == col_index % row_count
        relay = jnp.concatenate([relay_u, relay_v], axis=0).astype(jnp.float32)
        relay = jnp.where(relay_here, relay, jnp.zeros_like(relay))
        own_chol = jnp.where(row_index == diag_owner, own_chol, jnp.zeros_like(own_chol))
        merged = lax.psum(
            jnp.concatenate([own_chol, relay.reshape(-1, tile_order)], axis=0), "row"
        )
        chol_k = merged[:tile_order]
        relay = merged[tile_order:].reshape(relay.shape).astype(jnp.bfloat16)
        col_u = relay[:tiles_col]
        col_raw = relay[tiles_col:]
        solved = solve_packed(chol_k, jnp.concatenate([row_raw, col_raw], axis=0))
        row_v = solved[:tiles_row]
        col_v = solved[tiles_row:]
        row_live = (row_tile > panel_index)[:, None, None]
        col_live = (col_tile > panel_index)[:, None, None]
        row_u = jnp.where(row_live, row_u, zero_bf)
        row_v = jnp.where(row_live, row_v, zero_bf)
        col_u = jnp.where(col_live, col_u, zero_bf)
        col_v = jnp.where(col_live, col_v, zero_bf)
        self_c = jnp.einsum(
            "arx,asx->ars", row_v, row_v, preferred_element_type=jnp.float32
        ).astype(jnp.bfloat16)
        spread = jnp.einsum(
            "ars,asx->arx", self_c, row_u, preferred_element_type=jnp.float32
        ).astype(jnp.bfloat16)
        part_u = lax.dynamic_slice_in_dim(row_u, first_row, diag_rows, 2)
        lowered = diagonal - jnp.einsum(
            "arx,ary->axy", part_u, spread, preferred_element_type=jnp.float32
        )
        chol_rows = lax.dynamic_slice_in_dim(chol_k, first_row, diag_rows, 0)
        chol_rows = jnp.where(chol_cols <= chol_rows_at, chol_rows, 0.0)
        diag_tile = row_tile[:, None, None]
        diagonal = jnp.where(
            diag_tile > panel_index,
            lowered,
            jnp.where(diag_tile == panel_index, chol_rows[None], diagonal),
        )
        if panel_index + 1 < PANELS:
            next_slot = (panel_index + 1) // row_count
            whole_tile = lax.all_gather(diagonal[next_slot], "col", axis=0, tiled=True)
        coupling = jnp.einsum("arx,bsx->abrs", row_v, col_v, preferred_element_type=jnp.float32)
        col_sketch = jnp.einsum("rx,bsx->brs", sketch, col_u, preferred_element_type=jnp.float32)
        sketch_v = jnp.einsum(
            "rx,absx->abrs", sketch, factor_v, preferred_element_type=jnp.float32
        ).astype(jnp.bfloat16)
        sketch_c = jnp.einsum("brs,abts->abrt", col_sketch, coupling, precision=highest).astype(
            jnp.bfloat16
        )
        range_y = jnp.einsum(
            "abrs,absx->abrx", sketch_v, factor_u, preferred_element_type=jnp.float32
        )
        range_y = range_y - jnp.einsum(
            "abrs,asx->abrx", sketch_c, row_u, preferred_element_type=jnp.float32
        )
        keep_rows = rank_slots[None, None, :] < rank_levels[panel_index + 1][:, :, None]
        range_y = jnp.where(keep_rows[..., None], range_y, 0.0).astype(jnp.bfloat16)
        gram_matrix = jnp.einsum(
            "abrx,absx->abrs", range_y, range_y, preferred_element_type=jnp.float32
        )
        gram_matrix = gram_matrix + (1.0 - keep_rows.astype(jnp.float32))[..., None] * identity
        proj_u = jnp.einsum(
            "abrx,absx->abrs", range_y, factor_u, preferred_element_type=jnp.float32
        )
        proj_own = jnp.einsum("abrx,asx->abrs", range_y, row_u, preferred_element_type=jnp.float32)
        proj_c = jnp.einsum("abrs,abst->abrt", proj_own, coupling, precision=highest)
        gram_inv = factor_inverse(gram_matrix)
        both = jnp.concatenate([proj_u, proj_c], axis=-1)
        middle = jnp.einsum("abrs,abst->abrt", gram_inv, both, precision=highest)
        cores = jnp.einsum("absr,abst->abrt", gram_inv, middle, precision=highest)
        first_core = cores[..., :rank_width].astype(jnp.bfloat16)
        second_core = cores[..., rank_width:].astype(jnp.bfloat16)
        fresh_v = jnp.einsum(
            "abrs,absx->abrx", first_core, factor_v, preferred_element_type=jnp.float32
        )
        fresh_v = (
            fresh_v
            - jnp.einsum("abrs,bsx->abrx", second_core, col_u, preferred_element_type=jnp.float32)
        ).astype(jnp.bfloat16)
        if whole_tile is not None:
            whole_tile, fresh_v = lax.optimization_barrier((whole_tile, fresh_v))
        update_mask = ((row_tile[:, None] > col_tile[None, :]) & (col_tile[None, :] > panel_index))[
            ..., None, None
        ]
        at_panel = ((col_tile[None, :] == panel_index) & (row_tile[:, None] > panel_index))[
            ..., None, None
        ]
        factor_u = jnp.where(update_mask, range_y, jnp.where(at_panel, row_u[:, None], factor_u))
        factor_v = jnp.where(update_mask, fresh_v, jnp.where(at_panel, row_v[:, None], factor_v))
    return (factor_u, factor_v, diagonal)


def solution(mesh):
    in_specs = (
        P("row", "col", None, None),
        P("row", "col", None, None),
        P("row", "col", None),
        P(),
        P(None, "row", "col"),
    )
    out_specs = (P("row", "col", None, None), P("row", "col", None, None), P("row", "col", None))
    return jax.shard_map(
        on_device, mesh=mesh, in_specs=in_specs, out_specs=out_specs, check_vma=False
    )
```

```python
import jax
import jax.numpy as jnp
from jax import lax
from jax.sharding import PartitionSpec as P

PANELS = 2


highest = lax.Precision.HIGHEST
fine = lax.Precision.HIGH


def broadcast(shard, axis, root):
    mine = lax.axis_index(axis) == root
    return lax.psum(jnp.where(mine, shard, jnp.zeros_like(shard)), axis)


def chol_apply(factor, rhs):
    middle = jax.scipy.linalg.solve_triangular(factor, rhs, lower=True)
    return jax.scipy.linalg.solve_triangular(factor, middle, lower=True, trans=1)


def solve_panel(chol_k, raw_factors):
    tile_count, rank_width, tile_order = raw_factors.shape
    flattened = raw_factors.reshape(tile_count * rank_width, tile_order).astype(jnp.float32).T
    solved = jax.scipy.linalg.solve_triangular(chol_k, flattened, lower=True)
    return solved.T.reshape(tile_count, rank_width, tile_order).astype(jnp.bfloat16)


BLOCK = 128


def factor_tile(tile_mat):
    order = tile_mat.shape[0]
    width = min(BLOCK, order)
    count = order // width
    sym = (tile_mat + tile_mat.T) * 0.5
    eye = jnp.eye(width, dtype=jnp.float32)
    packed = jnp.zeros((order, order), jnp.float32)
    for step in range(count):
        lo, hi = step * width, (step + 1) * width
        column = sym[lo:, lo:hi]
        if step:
            column = column - jnp.dot(packed[lo:, :lo], packed[lo:hi, :lo].T, precision=fine)
        head = jnp.tril(lax.linalg.cholesky(column[:width], symmetrize_input=False))
        head_inv = lax.linalg.triangular_solve(head, eye, left_side=True, lower=True)
        block = head + jnp.triu(head_inv.T, 1)
        if step < count - 1:
            below = jnp.dot(column[width:], head_inv.T, precision=fine)
            block = jnp.concatenate([block, below], axis=0)
        packed = lax.dynamic_update_slice(packed, block, (lo, lo))
    return packed


def factor_inverse(gram):
    order = gram.shape[-1]
    width = min(BLOCK, order)
    gram = (gram + jnp.swapaxes(gram, -1, -2)) * 0.5
    eye = jnp.broadcast_to(jnp.eye(width, dtype=jnp.float32), gram.shape[:-2] + (width, width))
    head = jnp.tril(lax.linalg.cholesky(gram[..., :width, :width], symmetrize_input=False))
    head_inv = lax.linalg.triangular_solve(head, eye, left_side=True, lower=True)
    if width == order:
        return head_inv
    rest = order - width
    below = jnp.einsum("...ij,...kj->...ik", gram[..., width:, :width], head_inv, precision=fine)
    tail = gram[..., width:, width:] - jnp.einsum("...ij,...kj->...ik", below, below, precision=fine)
    tail = jnp.tril(lax.linalg.cholesky(tail, symmetrize_input=False))
    eye_rest = jnp.broadcast_to(jnp.eye(rest, dtype=jnp.float32), gram.shape[:-2] + (rest, rest))
    tail_inv = lax.linalg.triangular_solve(tail, eye_rest, left_side=True, lower=True)
    cross = jnp.einsum("...ij,...jk->...ik", below, head_inv, precision=fine)
    cross = -jnp.einsum("...ij,...jk->...ik", tail_inv, cross, precision=fine)
    top = jnp.concatenate([head_inv, jnp.zeros(gram.shape[:-2] + (width, rest), jnp.float32)], -1)
    return jnp.concatenate([top, jnp.concatenate([cross, tail_inv], -1)], -2)


def solve_packed(packed, raw_factors):
    order = packed.shape[0]
    width = min(BLOCK, order)
    count = order // width
    lead = raw_factors.shape[:-1]
    rest = raw_factors.reshape(-1, order).astype(jnp.float32)
    done = []
    for step in range(count):
        lo, hi = step * width, (step + 1) * width
        block = packed[lo:hi, lo:hi]
        inverse = jnp.tril(block.T, -1) + jnp.diag(1.0 / jnp.diagonal(block))
        part = jnp.dot(rest[:, :width], inverse.T, precision=fine)
        done.append(part)
        if step < count - 1:
            rest = rest[:, width:] - jnp.dot(part, packed[hi:, lo:hi].T, precision=fine)
    return jnp.concatenate(done, axis=1).reshape(lead + (order,)).astype(jnp.bfloat16)


def zero_tile(tile_mat):
    return jnp.zeros_like(tile_mat)


def zero_factors(chol_k, raw_factors):
    return jnp.zeros_like(raw_factors)


def on_device(u_factors, v_factors, diag_tiles, sketch, rank_levels):
    row_count = lax.axis_size("row")
    col_count = lax.axis_size("col")
    row_index = lax.axis_index("row")
    col_index = lax.axis_index("col")
    tiles_row, tiles_col, rank_width, tile_order = u_factors.shape
    diag_rows = diag_tiles.shape[1]
    col_ratio = col_count // row_count
    row_tile = jnp.arange(tiles_row, dtype=jnp.int32) * row_count + row_index
    col_tile = jnp.arange(tiles_col, dtype=jnp.int32) * col_count + col_index
    rank_slots = jnp.arange(rank_width, dtype=jnp.int32)
    identity = jnp.eye(rank_width, dtype=jnp.float32)
    zero_bf = jnp.zeros((), jnp.bfloat16)
    below_diag = row_tile[:, None] > col_tile[None, :]
    live_rows = (rank_slots[None, None, :] < rank_levels[0][:, :, None]) & below_diag[:, :, None]
    factor_u = jnp.where(live_rows[..., None], u_factors, zero_bf)
    factor_v = jnp.where(live_rows[..., None], v_factors, zero_bf)
    diagonal = diag_tiles
    first_row = col_index * diag_rows
    pick_slot = col_index // row_count
    chol_cols = jnp.arange(tile_order, dtype=jnp.int32)[None, :]
    chol_rows_at = first_row + jnp.arange(diag_rows, dtype=jnp.int32)[:, None]
    whole_tile = None
    for panel_index in range(PANELS):
        diag_slot = panel_index // row_count
        diag_owner = panel_index % row_count
        col_slot = panel_index // col_count
        col_owner = panel_index % col_count
        raw_u = factor_u[:, col_slot]
        raw_v = factor_v[:, col_slot]
        if whole_tile is None:
            whole_tile = lax.all_gather(diagonal[diag_slot], "col", axis=0, tiled=True)
            whole_tile, raw_u, raw_v = lax.optimization_barrier((whole_tile, raw_u, raw_v))
        row_u, row_raw = (
            broadcast(raw_u, "col", col_owner),
            broadcast(raw_v, "col", col_owner),
        )
        relay_u = lax.dynamic_index_in_dim(
            row_u.reshape(tiles_col, col_ratio, rank_width, tile_order),
            pick_slot,
            1,
            keepdims=False,
        )
        relay_v = lax.dynamic_index_in_dim(
            row_raw.reshape(tiles_col, col_ratio, rank_width, tile_order),
            pick_slot,
            1,
            keepdims=False,
        )
        own_chol = lax.cond(row_index == diag_owner, factor_tile, zero_tile, whole_tile)
        whole_tile = None
        relay_here = row_index == col_index % row_count
        relay = jnp.concatenate([relay_u, relay_v], axis=0).astype(jnp.float32)
        relay = jnp.where(relay_here, relay, jnp.zeros_like(relay))
        own_chol = jnp.where(row_index == diag_owner, own_chol, jnp.zeros_like(own_chol))
        merged = lax.psum(
            jnp.concatenate([own_chol, relay.reshape(-1, tile_order)], axis=0), "row"
        )
        chol_k = merged[:tile_order]
        relay = merged[tile_order:].reshape(relay.shape).astype(jnp.bfloat16)
        col_u = relay[:tiles_col]
        col_raw = relay[tiles_col:]
        solved = solve_packed(chol_k, jnp.concatenate([row_raw, col_raw], axis=0))
        row_v = solved[:tiles_row]
        col_v = solved[tiles_row:]
        row_live = (row_tile > panel_index)[:, None, None]
        col_live = (col_tile > panel_index)[:, None, None]
        row_u = jnp.where(row_live, row_u, zero_bf)
        row_v = jnp.where(row_live, row_v, zero_bf)
        col_u = jnp.where(col_live, col_u, zero_bf)
        col_v = jnp.where(col_live, col_v, zero_bf)
        self_c = jnp.einsum(
            "arx,asx->ars", row_v, row_v, preferred_element_type=jnp.float32
        ).astype(jnp.bfloat16)
        spread = jnp.einsum(
            "ars,asx->arx", self_c, row_u, preferred_element_type=jnp.float32
        ).astype(jnp.bfloat16)
        part_u = lax.dynamic_slice_in_dim(row_u, first_row, diag_rows, 2)
        lowered = diagonal - jnp.einsum(
            "arx,ary->axy", part_u, spread, preferred_element_type=jnp.float32
        )
        chol_rows = lax.dynamic_slice_in_dim(chol_k, first_row, diag_rows, 0)
        chol_rows = jnp.where(chol_cols <= chol_rows_at, chol_rows, 0.0)
        diag_tile = row_tile[:, None, None]
        diagonal = jnp.where(
            diag_tile > panel_index,
            lowered,
            jnp.where(diag_tile == panel_index, chol_rows[None], diagonal),
        )
        if panel_index + 1 < PANELS:
            next_slot = (panel_index + 1) // row_count
            whole_tile = lax.all_gather(diagonal[next_slot], "col", axis=0, tiled=True)
        coupling = jnp.einsum("arx,bsx->abrs", row_v, col_v, preferred_element_type=jnp.float32)
        col_sketch = jnp.einsum("rx,bsx->brs", sketch, col_u, preferred_element_type=jnp.float32)
        sketch_v = jnp.einsum(
            "rx,absx->abrs", sketch, factor_v, preferred_element_type=jnp.float32
        ).astype(jnp.bfloat16)
        sketch_c = jnp.einsum("brs,abts->abrt", col_sketch, coupling, precision=fine).astype(
            jnp.bfloat16
        )
        range_y = jnp.einsum(
            "abrs,absx->abrx", sketch_v, factor_u, preferred_element_type=jnp.float32
        )
        range_y = range_y - jnp.einsum(
            "abrs,asx->abrx", sketch_c, row_u, preferred_element_type=jnp.float32
        )
        keep_rows = rank_slots[None, None, :] < rank_levels[panel_index + 1][:, :, None]
        range_y = jnp.where(keep_rows[..., None], range_y, 0.0).astype(jnp.bfloat16)
        gram_matrix = jnp.einsum(
            "abrx,absx->abrs", range_y, range_y, preferred_element_type=jnp.float32
        )
        gram_matrix = gram_matrix + (1.0 - keep_rows.astype(jnp.float32))[..., None] * identity
        proj_u = jnp.einsum(
            "abrx,absx->abrs", range_y, factor_u, preferred_element_type=jnp.float32
        )
        proj_own = jnp.einsum("abrx,asx->abrs", range_y, row_u, preferred_element_type=jnp.float32)
        proj_c = jnp.einsum("abrs,abst->abrt", proj_own, coupling, precision=fine)
        gram_inv = factor_inverse(gram_matrix)
        both = jnp.concatenate([proj_u, proj_c], axis=-1)
        middle = jnp.einsum("abrs,abst->abrt", gram_inv, both, precision=fine)
        cores = jnp.einsum("absr,abst->abrt", gram_inv, middle, precision=fine)
        first_core = cores[..., :rank_width].astype(jnp.bfloat16)
        second_core = cores[..., rank_width:].astype(jnp.bfloat16)
        fresh_v = jnp.einsum(
            "abrs,absx->abrx", first_core, factor_v, preferred_element_type=jnp.float32
        )
        fresh_v = (
            fresh_v
            - jnp.einsum("abrs,bsx->abrx", second_core, col_u, preferred_element_type=jnp.float32)
        ).astype(jnp.bfloat16)
        if whole_tile is not None:
            whole_tile, fresh_v = lax.optimization_barrier((whole_tile, fresh_v))
        update_mask = ((row_tile[:, None] > col_tile[None, :]) & (col_tile[None, :] > panel_index))[
            ..., None, None
        ]
        at_panel = ((col_tile[None, :] == panel_index) & (row_tile[:, None] > panel_index))[
            ..., None, None
        ]
        factor_u = jnp.where(update_mask, range_y, jnp.where(at_panel, row_u[:, None], factor_u))
        factor_v = jnp.where(update_mask, fresh_v, jnp.where(at_panel, row_v[:, None], factor_v))
    return (factor_u, factor_v, diagonal)


def solution(mesh):
    in_specs = (
        P("row", "col", None, None),
        P("row", "col", None, None),
        P("row", "col", None),
        P(),
        P(None, "row", "col"),
    )
    out_specs = (P("row", "col", None, None), P("row", "col", None, None), P("row", "col", None))
    return jax.shard_map(
        on_device, mesh=mesh, in_specs=in_specs, out_specs=out_specs, check_vma=False
    )
```

```python
import jax
import jax.numpy as jnp
from jax import lax
from jax.sharding import PartitionSpec as P

PANELS = 2


highest = lax.Precision.HIGHEST
fine = lax.Precision.HIGH


def broadcast(shard, axis, root):
    mine = lax.axis_index(axis) == root
    return lax.psum(jnp.where(mine, shard, jnp.zeros_like(shard)), axis)


def chol_apply(factor, rhs):
    middle = jax.scipy.linalg.solve_triangular(factor, rhs, lower=True)
    return jax.scipy.linalg.solve_triangular(factor, middle, lower=True, trans=1)


def solve_panel(chol_k, raw_factors):
    tile_count, rank_width, tile_order = raw_factors.shape
    flattened = raw_factors.reshape(tile_count * rank_width, tile_order).astype(jnp.float32).T
    solved = jax.scipy.linalg.solve_triangular(chol_k, flattened, lower=True)
    return solved.T.reshape(tile_count, rank_width, tile_order).astype(jnp.bfloat16)


BLOCK = 128


def factor_tile(tile_mat):
    order = tile_mat.shape[0]
    width = min(BLOCK, order)
    count = order // width
    sym = (tile_mat + tile_mat.T) * 0.5
    eye = jnp.eye(width, dtype=jnp.float32)
    packed = jnp.zeros((order, order), jnp.float32)
    for step in range(count):
        lo, hi = step * width, (step + 1) * width
        column = sym[lo:, lo:hi]
        if step:
            column = column - jnp.dot(packed[lo:, :lo], packed[lo:hi, :lo].T, precision=fine)
        head = jnp.tril(lax.linalg.cholesky(column[:width], symmetrize_input=False))
        head_inv = lax.linalg.triangular_solve(head, eye, left_side=True, lower=True)
        block = head + jnp.triu(head_inv.T, 1)
        if step < count - 1:
            below = jnp.dot(column[width:], head_inv.T, precision=fine)
            block = jnp.concatenate([block, below], axis=0)
        packed = lax.dynamic_update_slice(packed, block, (lo, lo))
    return packed


def factor_inverse(gram):
    order = gram.shape[-1]
    width = min(BLOCK, order)
    gram = (gram + jnp.swapaxes(gram, -1, -2)) * 0.5
    eye = jnp.broadcast_to(jnp.eye(width, dtype=jnp.float32), gram.shape[:-2] + (width, width))
    head = jnp.tril(lax.linalg.cholesky(gram[..., :width, :width], symmetrize_input=False))
    head_inv = lax.linalg.triangular_solve(head, eye, left_side=True, lower=True)
    if width == order:
        return head_inv
    rest = order - width
    below = jnp.einsum("...ij,...kj->...ik", gram[..., width:, :width], head_inv, precision=highest)
    tail = gram[..., width:, width:] - jnp.einsum("...ij,...kj->...ik", below, below, precision=highest)
    tail = jnp.tril(lax.linalg.cholesky(tail, symmetrize_input=False))
    eye_rest = jnp.broadcast_to(jnp.eye(rest, dtype=jnp.float32), gram.shape[:-2] + (rest, rest))
    tail_inv = lax.linalg.triangular_solve(tail, eye_rest, left_side=True, lower=True)
    cross = jnp.einsum("...ij,...jk->...ik", below, head_inv, precision=highest)
    cross = -jnp.einsum("...ij,...jk->...ik", tail_inv, cross, precision=highest)
    top = jnp.concatenate([head_inv, jnp.zeros(gram.shape[:-2] + (width, rest), jnp.float32)], -1)
    return jnp.concatenate([top, jnp.concatenate([cross, tail_inv], -1)], -2)


def solve_packed(packed, raw_factors):
    order = packed.shape[0]
    width = min(BLOCK, order)
    count = order // width
    lead = raw_factors.shape[:-1]
    rest = raw_factors.reshape(-1, order).astype(jnp.float32)
    blocks = jnp.stack([packed[s * width:(s + 1) * width, s * width:(s + 1) * width] for s in range(count)])
    eye = jnp.eye(width, dtype=jnp.bool_)
    lower = jnp.arange(width)[:, None] > jnp.arange(width)[None, :]
    inverses = jnp.where(lower, jnp.swapaxes(blocks, -1, -2), 0.0) + jnp.where(
        eye, 1.0 / jnp.where(eye, blocks, 1.0), 0.0
    )
    done = []
    for step in range(count):
        lo, hi = step * width, (step + 1) * width
        part = jnp.dot(rest[:, :width], inverses[step].T, precision=fine)
        done.append(part)
        if step < count - 1:
            rest = rest[:, width:] - jnp.dot(part, packed[hi:, lo:hi].T, precision=fine)
    return jnp.concatenate(done, axis=1).reshape(lead + (order,)).astype(jnp.bfloat16)


def zero_tile(tile_mat):
    return jnp.zeros_like(tile_mat)


def zero_factors(chol_k, raw_factors):
    return jnp.zeros_like(raw_factors)


def on_device(u_factors, v_factors, diag_tiles, sketch, rank_levels):
    row_count = lax.axis_size("row")
    col_count = lax.axis_size("col")
    row_index = lax.axis_index("row")
    col_index = lax.axis_index("col")
    tiles_row, tiles_col, rank_width, tile_order = u_factors.shape
    diag_rows = diag_tiles.shape[1]
    col_ratio = col_count // row_count
    row_tile = jnp.arange(tiles_row, dtype=jnp.int32) * row_count + row_index
    col_tile = jnp.arange(tiles_col, dtype=jnp.int32) * col_count + col_index
    rank_slots = jnp.arange(rank_width, dtype=jnp.int32)
    identity = jnp.eye(rank_width, dtype=jnp.float32)
    zero_bf = jnp.zeros((), jnp.bfloat16)
    below_diag = row_tile[:, None] > col_tile[None, :]
    live_rows = (rank_slots[None, None, :] < rank_levels[0][:, :, None]) & below_diag[:, :, None]
    factor_u = jnp.where(live_rows[..., None], u_factors, zero_bf)
    factor_v = jnp.where(live_rows[..., None], v_factors, zero_bf)
    diagonal = diag_tiles
    first_row = col_index * diag_rows
    pick_slot = col_index // row_count
    chol_cols = jnp.arange(tile_order, dtype=jnp.int32)[None, :]
    chol_rows_at = first_row + jnp.arange(diag_rows, dtype=jnp.int32)[:, None]
    whole_tile = None
    for panel_index in range(PANELS):
        diag_slot = panel_index // row_count
        diag_owner = panel_index % row_count
        col_slot = panel_index // col_count
        col_owner = panel_index % col_count
        raw_u = factor_u[:, col_slot]
        raw_v = factor_v[:, col_slot]
        if whole_tile is None:
            whole_tile = lax.all_gather(diagonal[diag_slot], "col", axis=0, tiled=True)
            whole_tile, raw_u, raw_v = lax.optimization_barrier((whole_tile, raw_u, raw_v))
        row_u, row_raw = (
            broadcast(raw_u, "col", col_owner),
            broadcast(raw_v, "col", col_owner),
        )
        relay_u = lax.dynamic_index_in_dim(
            row_u.reshape(tiles_col, col_ratio, rank_width, tile_order),
            pick_slot,
            1,
            keepdims=False,
        )
        relay_v = lax.dynamic_index_in_dim(
            row_raw.reshape(tiles_col, col_ratio, rank_width, tile_order),
            pick_slot,
            1,
            keepdims=False,
        )
        own_chol = lax.cond(row_index == diag_owner, factor_tile, zero_tile, whole_tile)
        whole_tile = None
        relay_here = row_index == col_index % row_count
        relay = jnp.concatenate([relay_u, relay_v], axis=0).astype(jnp.float32)
        relay = jnp.where(relay_here, relay, jnp.zeros_like(relay))
        own_chol = jnp.where(row_index == diag_owner, own_chol, jnp.zeros_like(own_chol))
        merged = lax.psum(
            jnp.concatenate([own_chol, relay.reshape(-1, tile_order)], axis=0), "row"
        )
        chol_k = merged[:tile_order]
        relay = merged[tile_order:].reshape(relay.shape).astype(jnp.bfloat16)
        col_u = relay[:tiles_col]
        col_raw = relay[tiles_col:]
        solved = solve_packed(chol_k, jnp.concatenate([row_raw, col_raw], axis=0))
        row_v = solved[:tiles_row]
        col_v = solved[tiles_row:]
        row_live = (row_tile > panel_index)[:, None, None]
        col_live = (col_tile > panel_index)[:, None, None]
        row_u = jnp.where(row_live, row_u, zero_bf)
        row_v = jnp.where(row_live, row_v, zero_bf)
        col_u = jnp.where(col_live, col_u, zero_bf)
        col_v = jnp.where(col_live, col_v, zero_bf)
        self_c = jnp.einsum(
            "arx,asx->ars", row_v, row_v, preferred_element_type=jnp.float32
        ).astype(jnp.bfloat16)
        spread = jnp.einsum(
            "ars,asx->arx", self_c, row_u, preferred_element_type=jnp.float32
        ).astype(jnp.bfloat16)
        part_u = lax.dynamic_slice_in_dim(row_u, first_row, diag_rows, 2)
        lowered = diagonal - jnp.einsum(
            "arx,ary->axy", part_u, spread, preferred_element_type=jnp.float32
        )
        chol_rows = lax.dynamic_slice_in_dim(chol_k, first_row, diag_rows, 0)
        chol_rows = jnp.where(chol_cols <= chol_rows_at, chol_rows, 0.0)
        diag_tile = row_tile[:, None, None]
        diagonal = jnp.where(
            diag_tile > panel_index,
            lowered,
            jnp.where(diag_tile == panel_index, chol_rows[None], diagonal),
        )
        if panel_index + 1 < PANELS:
            next_slot = (panel_index + 1) // row_count
            whole_tile = lax.all_gather(diagonal[next_slot], "col", axis=0, tiled=True)
        coupling = jnp.einsum("arx,bsx->abrs", row_v, col_v, preferred_element_type=jnp.float32)
        col_sketch = jnp.einsum("rx,bsx->brs", sketch, col_u, preferred_element_type=jnp.float32)
        sketch_v = jnp.einsum(
            "rx,absx->abrs", sketch, factor_v, preferred_element_type=jnp.float32
        ).astype(jnp.bfloat16)
        sketch_c = jnp.einsum("brs,abts->abrt", col_sketch, coupling, precision=highest).astype(
            jnp.bfloat16
        )
        range_y = jnp.einsum(
            "abrs,absx->abrx", sketch_v, factor_u, preferred_element_type=jnp.float32
        )
        range_y = range_y - jnp.einsum(
            "abrs,asx->abrx", sketch_c, row_u, preferred_element_type=jnp.float32
        )
        keep_rows = rank_slots[None, None, :] < rank_levels[panel_index + 1][:, :, None]
        range_y = jnp.where(keep_rows[..., None], range_y, 0.0).astype(jnp.bfloat16)
        gram_matrix = jnp.einsum(
            "abrx,absx->abrs", range_y, range_y, preferred_element_type=jnp.float32
        )
        gram_matrix = gram_matrix + (1.0 - keep_rows.astype(jnp.float32))[..., None] * identity
        proj_u = jnp.einsum(
            "abrx,absx->abrs", range_y, factor_u, preferred_element_type=jnp.float32
        )
        proj_own = jnp.einsum("abrx,asx->abrs", range_y, row_u, preferred_element_type=jnp.float32)
        proj_c = jnp.einsum("abrs,abst->abrt", proj_own, coupling, precision=highest)
        gram_inv = factor_inverse(gram_matrix)
        both = jnp.concatenate([proj_u, proj_c], axis=-1)
        middle = jnp.einsum("abrs,abst->abrt", gram_inv, both, precision=highest)
        cores = jnp.einsum("absr,abst->abrt", gram_inv, middle, precision=highest)
        first_core = cores[..., :rank_width].astype(jnp.bfloat16)
        second_core = cores[..., rank_width:].astype(jnp.bfloat16)
        fresh_v = jnp.einsum(
            "abrs,absx->abrx", first_core, factor_v, preferred_element_type=jnp.float32
        )
        fresh_v = (
            fresh_v
            - jnp.einsum("abrs,bsx->abrx", second_core, col_u, preferred_element_type=jnp.float32)
        ).astype(jnp.bfloat16)
        if whole_tile is not None:
            whole_tile, fresh_v = lax.optimization_barrier((whole_tile, fresh_v))
        update_mask = ((row_tile[:, None] > col_tile[None, :]) & (col_tile[None, :] > panel_index))[
            ..., None, None
        ]
        at_panel = ((col_tile[None, :] == panel_index) & (row_tile[:, None] > panel_index))[
            ..., None, None
        ]
        factor_u = jnp.where(update_mask, range_y, jnp.where(at_panel, row_u[:, None], factor_u))
        factor_v = jnp.where(update_mask, fresh_v, jnp.where(at_panel, row_v[:, None], factor_v))
    return (factor_u, factor_v, diagonal)


def solution(mesh):
    in_specs = (
        P("row", "col", None, None),
        P("row", "col", None, None),
        P("row", "col", None),
        P(),
        P(None, "row", "col"),
    )
    out_specs = (P("row", "col", None, None), P("row", "col", None, None), P("row", "col", None))
    return jax.shard_map(
        on_device, mesh=mesh, in_specs=in_specs, out_specs=out_specs, check_vma=False
    )
```
